768 devices in a mesh: sect: 8 (over x, core), tile: 96 (over z, y).
Axes of the slice: x: 4, y: 8, z: 12, core: 2. Of those that a mesh axis runs over, the one named last changes fastest.
Arguments:
- spectrum: float32 [1296, 768, 128], P('sect', 'tile'), may hold values from 0.05 to 1
- courant: float32 [36], replicated, may hold values from 0.1 to 0.45
- group_ratio: float32 [36], replicated, may hold values from 0.5 to 1
- ocean_currents: float32 [2, 196608], P(None, 'tile'), may hold values from -0.15 to 0.15
- elevation: float32 [196608], P('tile'), may hold values from -0.5 to 0.5
- sea_mask: int32 [768, 128], P('tile'), may hold values 0 or 1
- owner_tile: int32 [98304, 1], P('tile'), may hold values from 0 to 95; in each aligned block of 1024 rows (0 to 1023, 1024 to 2047, ...) at most 22 rows name the same one
- ocean_slot: int32 [98304], P('tile'), may hold values from 0 to 2047
Outputs:
- new_spectrum: float32 [1296, 768, 128], P('sect', 'tile')
- ocean_stress: float32 [3, 196608], P(None, 'tile')
The draws below stay inside these ranges and needn't reach their ends.
Inputs may be any that keep to these rules, and one draw needn't show every extreme that they name: `owner_tile`: among the wave cells of one tile at most 22 name the same owner tile, a bound that some block reaches of them.
All inputs are finite; a program needn't handle non-finite values. No bound on the sum of `sea_mask` on one device may be relied on, other than what follows from the above.
Results may differ from the reference program's by a relative error of at most 0.00011.
Values sent between devices are 32-bit elements; how exact they have to be, the bound alone decides.
No kernel may reach another device: no remote copies, remote signals or barrier semaphores. Data moves between devices by JAX's collectives and lax.ppermute only.
A program may use at most 32 MiB of HBM per device.

```python
import math
import jax
import jax.numpy as jnp
import numpy as np
from jax import lax

NDIR = 36
NFREQ = 36
STEPS = 4
ROWS = 8
NX = 128
OCT = 2048
BINS = 1296
TILES = 96
NY = 768
CAP = 22
OCEAN = 196608


def place_ends(array, key, least, top_value):
    index_at = [jax.random.randint(jax.random.fold_in(key, axis), (), 0, length) for axis, length in enumerate(array.shape)]
    widest = array.shape.index(max(array.shape))
    beside = index_at[:widest] + [(index_at[widest] + 1) % array.shape[widest]] + index_at[widest + 1:]
    return array.at[tuple(index_at)].set(least).at[tuple(beside)].set(top_value)


def shard_levels(own_key, extent, shards, least, top_value):
    loudness, own = 1.0, jax.random.fold_in(own_key, 6)
    for dim, shards_of in shards:
        heights = jnp.exp(jax.random.uniform(jax.random.fold_in(own, dim), (shards_of,), jnp.float32, least / len(shards), top_value / len(shards)))
        loudness = loudness * jnp.repeat(heights, extent[dim] // shards_of).reshape([-1 if axis == dim else 1 for axis in range(len(extent))])
    return loudness


def assign_block(key, own, number, rows, number_of, top, most, skew):
    order = jax.random.permutation(key, number_of)
    packed, common = shares(number_of, rows * top, most, skew, True), shares(number_of, rows * top, most, skew, False)
    places = jnp.arange(number_of)

    def named(sizes, turn):
        used = int((sizes > 0).sum())
        fixed = max(1, used // 4)
        shifted = fixed + (places - fixed + turn * (used - fixed)) % max(1, number_of - fixed)
        return jnp.zeros((number_of,), jnp.int32).at[order[jnp.where(places < fixed, places, shifted)]].set(jnp.asarray(sizes, jnp.int32))

    sizes = jnp.where(number % 4 == 0, named(packed, number // 4), named(common, number - number // 4 - 1))
    mixed = jax.random.permutation(jax.random.fold_in(own, 3), number_of)
    giver, receiver = mixed[0:number_of // 2 * 2:2], mixed[1:number_of // 2 * 2:2]
    margin = jnp.minimum(sizes[giver] - 1, most - sizes[receiver]) // 2
    margin = jnp.where((giver == order[0]) | (receiver == order[0]) | (sizes[receiver] == 0), 0, jnp.maximum(margin, 0))
    shifted = jax.random.randint(jax.random.fold_in(own, 4), (number_of // 2,), 0, 1 << 20) % (margin + 1)
    sizes = sizes.at[giver].add(-shifted).at[receiver].add(shifted)
    members = jnp.searchsorted(jnp.cumsum(sizes), jnp.arange(rows * top), side="right").astype(jnp.int32)
    table = members.reshape(top, rows).T
    table = table[jax.random.permutation(jax.random.fold_in(own, 1), rows)]
    turn = jax.random.randint(jax.random.fold_in(own, 2), (rows, 1), 0, top)
    return jnp.take_along_axis(table, (jnp.arange(top)[None, :] + turn) % top, axis=1)


def shares(amount, total, reach, lean, full):
    loads = [(1 << 20) // math.isqrt(grade ** lean) + 1 for grade in range(1, amount + 1)]
    largest = reach if full else min(reach, max(-(-total // amount), total * loads[0] // sum(loads)))
    least = 1 if total - largest >= amount - 1 else 0
    holding, surplus = [largest] + [least] * (amount - 1), total - largest - least * (amount - 1)
    while surplus > 0:
        candidates = [i for i in range(1, amount) if holding[i] < largest] or [i for i in range(1, amount) if holding[i] < reach]
        pool, left = sum([loads[i] for i in candidates]), surplus
        for i in candidates:
            addition = min(reach - holding[i], max(1, left * loads[i] // pool), surplus)
            holding[i] = holding[i] + addition
            surplus = surplus - addition
    return np.array(holding)


def setup_inputs(seed: int = 0) -> dict:
    splits = jax.random.split(jax.random.key(seed), 9)
    spectrum = jnp.clip(jnp.exp(math.log(1.0) - 2.9957323 * jax.random.uniform(splits[0], (BINS, NY, NX), jnp.float32) ** shard_levels(splits[0], (BINS, NY, NX), ((0, 8), (1, 96)), -0.2, 0.2)), 0.05, 1.0)
    courant = jnp.clip(jnp.exp(jax.random.uniform(splits[1], (NFREQ,), jnp.float32, math.log(0.1), math.log(0.45))), 0.1, 0.45)
    group_ratio = jnp.clip(jax.random.uniform(splits[2], (NFREQ,), jnp.float32, 0.5, 1.0), 0.5, 1.0)
    ocean_currents = jnp.clip(jax.random.uniform(splits[3], (2, OCEAN), jnp.float32, -0.15, 0.15) * shard_levels(splits[3], (2, OCEAN), ((1, 96),), -0.4, 0.0), -0.15, 0.15)
    elevation = jnp.clip(jax.random.uniform(splits[4], (OCEAN,), jnp.float32, -0.5, 0.5) * shard_levels(splits[4], (OCEAN,), ((0, 96),), -0.4, 0.0), -0.5, 0.5)
    sea_mask = place_ends((jax.random.randint(splits[5], (NY, NX), 0, 4) < 3).astype(jnp.int32), jax.random.fold_in(splits[5], 1), 0, 1)
    owner_tile_keys = jax.random.split(jax.random.fold_in(splits[6], 1), (NY * NX) // (ROWS * NX))
    owner_tile_turns = jax.random.permutation(jax.random.fold_in(splits[6], 3), (NY * NX) // (ROWS * NX))
    owner_tile = jax.vmap(lambda own, number: assign_block(jax.random.fold_in(splits[6], 2), own, number, ROWS * NX, TILES, 1, CAP, 2))(owner_tile_keys, owner_tile_turns).reshape((NY * NX, 1))
    ocean_slot = place_ends(jax.random.randint(splits[7], (NY * NX,), 0, OCT), jax.random.fold_in(splits[7], 1), 0, OCT - 1).astype(jnp.int32)
    return {"spectrum": spectrum, "courant": courant, "group_ratio": group_ratio, "ocean_currents": ocean_currents, "elevation": elevation, "sea_mask": sea_mask, "owner_tile": owner_tile, "ocean_slot": ocean_slot}


def advance(energy, flow_fields, speed_x, speed_y):
    vel_x = speed_x + flow_fields[0]
    vel_y = speed_y + flow_fields[1]
    middle = energy[:, 1:-1]
    mid_vel = vel_x[:, 1:-1]
    face_x = 0.5 * (mid_vel + jnp.roll(mid_vel, -1, axis=2))
    east_side = jnp.roll(middle, -1, axis=2)
    flux_x = jnp.maximum(face_x, 0.0) * middle + jnp.minimum(face_x, 0.0) * east_side
    div_x = flux_x - jnp.roll(flux_x, 1, axis=2)
    face_y = 0.5 * (vel_y[:, :-1] + vel_y[:, 1:])
    flux_y = jnp.maximum(face_y, 0.0) * energy[:, :-1] + jnp.minimum(face_y, 0.0) * energy[:, 1:]
    div_y = flux_y[:, 1:] - flux_y[:, :-1]
    return flow_fields[2, 1:-1] * (middle - div_x - div_y)


def reference(spectrum, courant, group_ratio, ocean_currents, elevation, sea_mask, owner_tile, ocean_slot):
    target = (owner_tile[:, 0] * OCT + ocean_slot).astype(jnp.int32)
    current_at = ocean_currents[:, target]
    eta_at = elevation[target]
    sea_float = sea_mask.astype(jnp.float32)
    flow_fields = jnp.concatenate([current_at.reshape(2, NY, NX), sea_float[None]], 0)
    flow_padded = jnp.pad(flow_fields, ((0, 0), (1, 1), (0, 0)))
    energy = spectrum.reshape(NDIR, NFREQ, NY, NX)

    def one_direction(pieces):
        spectra, dir_id = pieces
        angles = (dir_id.astype(jnp.float32) + 0.5) * (2.0 * math.pi / NDIR)
        cos_dir = jnp.cos(angles)
        sin_dir = jnp.sin(angles)
        speed_x = (courant * cos_dir)[:, None, None]
        speed_y = (courant * sin_dir)[:, None, None]
        for sub_step in range(STEPS):
            spectra = advance(jnp.pad(spectra, ((0, 0), (1, 1), (0, 0))), flow_padded, speed_x, speed_y)
        weights = jnp.stack([group_ratio * (1.0 + cos_dir * cos_dir) - 0.5,
                             group_ratio * cos_dir * sin_dir,
                             group_ratio * (1.0 + sin_dir * sin_dir) - 0.5], 0) * (4.0 / (NDIR * NFREQ))
        partial_value = jnp.dot(weights, spectra.reshape(NFREQ, NY * NX), precision=lax.Precision.HIGHEST)
        return spectra, partial_value

    spectra_all, partials = lax.map(one_direction, (energy, jnp.arange(NDIR, dtype=jnp.int32)))
    stress_w = jnp.sum(partials, 0) * ((1.0 + eta_at) * sea_float.reshape(-1))
    totals = jax.ops.segment_sum(stress_w.T, target, num_segments=OCEAN)
    counts = jax.ops.segment_sum(jnp.ones((NY * NX,), jnp.float32), target, num_segments=OCEAN)
    ocean_stress = (totals / jnp.maximum(counts, 1.0)[:, None]).T
    return spectra_all.reshape(NDIR * NFREQ, NY, NX), ocean_stress
```

```python
import math

import jax
import jax.numpy as jnp
from jax import lax
from jax.sharding import PartitionSpec as P

NDIR = 36
NFREQ = 36
STEPS = 4


def with_halo(x, sides, width):
    for axis, dim in sides:
        size, length = (lax.axis_size(axis), x.shape[dim])
        up = [(i, (i + 1) % size) for i in range(size - 1)]
        down = [(j, i) for i, j in up]
        last = lax.slice_in_dim(x, length - width, length, axis=dim)
        leading = lax.slice_in_dim(x, 0, width, axis=dim)
        before = lax.ppermute(last, axis, up)
        after = lax.ppermute(leading, axis, down)
        x = jnp.concatenate([before, x, after], axis=dim)
    return x


def advance(energy, flow_fields, speed_x, speed_y):
    vel_x = speed_x + flow_fields[0]
    vel_y = speed_y + flow_fields[1]
    middle = energy[:, 1:-1]
    mid_vel = vel_x[:, 1:-1]
    face_x = 0.5 * (mid_vel + jnp.roll(mid_vel, -1, axis=2))
    east_side = jnp.roll(middle, -1, axis=2)
    flux_x = jnp.maximum(face_x, 0.0) * middle + jnp.minimum(face_x, 0.0) * east_side
    div_x = flux_x - jnp.roll(flux_x, 1, axis=2)
    face_y = 0.5 * (vel_y[:, :-1] + vel_y[:, 1:])
    flux_y = jnp.maximum(face_y, 0.0) * energy[:, :-1] + jnp.minimum(face_y, 0.0) * energy[:, 1:]
    div_y = flux_y[:, 1:] - flux_y[:, :-1]
    return flow_fields[2, 1:-1] * (middle - div_x - div_y)


def local(
    spectrum, courant, group_ratio, ocean_currents, elevation, sea_mask, owner_tile, ocean_slot
):
    bin_count, row_count, columns = spectrum.shape
    cell_count = row_count * columns
    tile_count = lax.axis_size("tile")
    capacity = 2 * ((cell_count + tile_count - 1) // tile_count)
    ocean_cells = elevation.shape[0]
    first_bin = lax.axis_index("sect") * bin_count
    bin_ids = first_bin + jnp.arange(bin_count, dtype=jnp.int32)
    dir_ids = bin_ids // NFREQ
    freq_ids = bin_ids % NFREQ
    freq_pick = (freq_ids[:, None] == jnp.arange(NFREQ, dtype=jnp.int32)[None, :]).astype(
        jnp.float32
    )
    group_speed = jnp.sum(freq_pick * courant[None, :], 1)
    ratio_bin = jnp.sum(freq_pick * group_ratio[None, :], 1)
    angles = (dir_ids.astype(jnp.float32) + 0.5) * (2.0 * math.pi / NDIR)
    cos_dir = jnp.cos(angles)
    sin_dir = jnp.sin(angles)
    speed_x = (group_speed * cos_dir)[:, None, None]
    speed_y = (group_speed * sin_dir)[:, None, None]
    owners = owner_tile[:, 0]
    cell_ids = jnp.arange(owners.shape[0], dtype=jnp.int32)
    same_before = (owners[None, :] == owners[:, None]) & (cell_ids[None, :] < cell_ids[:, None])
    rank_in = jnp.sum(same_before.astype(jnp.int32), 1)
    position = owners * capacity + rank_in
    requests = jnp.full((tile_count * capacity,), -1, jnp.int32).at[position].set(ocean_slot)
    asked_slots = lax.all_to_all(
        requests.reshape(tile_count, capacity), "tile", split_axis=0, concat_axis=0, tiled=True
    )
    is_valid = asked_slots >= 0
    slot_index = jnp.where(is_valid, asked_slots, 0)
    surface = jnp.concatenate([ocean_currents, elevation[None]], 0)
    answer = jnp.where(is_valid[None], surface[:, slot_index], 0.0)
    returned = lax.all_to_all(answer, "tile", split_axis=1, concat_axis=1, tiled=True)
    at_cells = returned.reshape(3, tile_count * capacity)[:, position]
    sea_float = sea_mask.astype(jnp.float32)
    flow_fields = jnp.concatenate([at_cells[:2].reshape(2, row_count, columns), sea_float[None]], 0)
    extended = with_halo(jnp.concatenate([spectrum, flow_fields], 0), (("tile", 1),), STEPS)
    energy = extended[:bin_count]
    for sub_step in range(STEPS):
        flows_now = extended[bin_count:, sub_step : extended.shape[1] - sub_step]
        energy = advance(energy, flows_now, speed_x, speed_y)
    weights = jnp.stack(
        [
            ratio_bin * (1.0 + cos_dir * cos_dir) - 0.5,
            ratio_bin * cos_dir * sin_dir,
            ratio_bin * (1.0 + sin_dir * sin_dir) - 0.5,
        ],
        0,
    ) * (4.0 / (NDIR * NFREQ))
    partial_value = jnp.dot(
        weights, energy.reshape(bin_count, cell_count), precision=lax.Precision.HIGHEST
    )
    partial_value = partial_value * ((1.0 + at_cells[2]) * sea_float.reshape(-1))
    partial_value = lax.psum(partial_value, "sect")
    packed = jnp.zeros((3, tile_count * capacity), jnp.float32).at[:, position].set(partial_value)
    arrived = lax.all_to_all(
        packed.reshape(3, tile_count, capacity), "tile", split_axis=1, concat_axis=1, tiled=True
    )
    flat_index = slot_index.reshape(-1)
    weight = is_valid.reshape(-1).astype(jnp.float32)
    totals = (
        jnp.zeros((3, ocean_cells), jnp.float32)
        .at[:, flat_index]
        .add(arrived.reshape(3, -1) * weight[None])
    )
    counts = jnp.zeros((ocean_cells,), jnp.float32).at[flat_index].add(weight)
    return (energy, totals / jnp.maximum(counts, 1.0)[None])


def solution(mesh):
    in_specs = (
        P("sect", "tile", None),
        P(),
        P(),
        P(None, "tile"),
        P("tile"),
        P("tile", None),
        P("tile", None),
        P("tile"),
    )
    out_specs = (P("sect", "tile", None), P(None, "tile"))
    return jax.shard_map(local, mesh=mesh, in_specs=in_specs, out_specs=out_specs, check_vma=False)
```

```python
import math

import jax
import jax.numpy as jnp
from jax import lax
from jax.sharding import PartitionSpec as P

NDIR = 36
NFREQ = 36
STEPS = 4


def with_halo(x, sides, width):
    for axis, dim in sides:
        size, length = (lax.axis_size(axis), x.shape[dim])
        up = [(i, (i + 1) % size) for i in range(size - 1)]
        down = [(j, i) for i, j in up]
        last = lax.slice_in_dim(x, length - width, length, axis=dim)
        leading = lax.slice_in_dim(x, 0, width, axis=dim)
        before = lax.ppermute(last, axis, up)
        after = lax.ppermute(leading, axis, down)
        x = jnp.concatenate([before, x, after], axis=dim)
    return x


def advance(energy, flow_fields, speed_x, speed_y):
    vel_x = speed_x + flow_fields[0]
    vel_y = speed_y + flow_fields[1]
    middle = energy[:, 1:-1]
    mid_vel = vel_x[:, 1:-1]
    face_x = 0.5 * (mid_vel + jnp.roll(mid_vel, -1, axis=2))
    east_side = jnp.roll(middle, -1, axis=2)
    flux_x = jnp.maximum(face_x, 0.0) * middle + jnp.minimum(face_x, 0.0) * east_side
    div_x = flux_x - jnp.roll(flux_x, 1, axis=2)
    face_y = 0.5 * (vel_y[:, :-1] + vel_y[:, 1:])
    flux_y = jnp.maximum(face_y, 0.0) * energy[:, :-1] + jnp.minimum(face_y, 0.0) * energy[:, 1:]
    div_y = flux_y[:, 1:] - flux_y[:, :-1]
    return flow_fields[2, 1:-1] * (middle - div_x - div_y)


def local(
    spectrum, courant, group_ratio, ocean_currents, elevation, sea_mask, owner_tile, ocean_slot
):
    bin_count, row_count, columns = spectrum.shape
    cell_count = row_count * columns
    ocean_cells = elevation.shape[0]
    first_bin = lax.axis_index("sect") * bin_count
    bin_ids = first_bin + jnp.arange(bin_count, dtype=jnp.int32)
    dir_ids = bin_ids // NFREQ
    freq_ids = bin_ids % NFREQ
    freq_pick = (freq_ids[:, None] == jnp.arange(NFREQ, dtype=jnp.int32)[None, :]).astype(
        jnp.float32
    )
    group_speed = jnp.sum(freq_pick * courant[None, :], 1)
    ratio_bin = jnp.sum(freq_pick * group_ratio[None, :], 1)
    angles = (dir_ids.astype(jnp.float32) + 0.5) * (2.0 * math.pi / NDIR)
    cos_dir = jnp.cos(angles)
    sin_dir = jnp.sin(angles)
    speed_x = (group_speed * cos_dir)[:, None, None]
    speed_y = (group_speed * sin_dir)[:, None, None]
    target = owner_tile[:, 0] * ocean_cells + ocean_slot
    surface = jnp.concatenate([ocean_currents, elevation[None]], 0)
    tile_count = lax.axis_size("tile")
    surface_all = lax.all_gather(surface.reshape(1, 3, -1, columns), "tile", axis=0, tiled=True)
    at_cells = jnp.stack([surface_all[:, k].reshape(-1)[target] for k in range(3)], 0)
    sea_float = sea_mask.astype(jnp.float32)
    flow_fields = jnp.concatenate([at_cells[:2].reshape(2, row_count, columns), sea_float[None]], 0)
    extended = with_halo(jnp.concatenate([spectrum, flow_fields], 0), (("tile", 1),), STEPS)
    energy = extended[:bin_count]
    for sub_step in range(STEPS):
        flows_now = extended[bin_count:, sub_step : extended.shape[1] - sub_step]
        energy = advance(energy, flows_now, speed_x, speed_y)
    weights = jnp.stack(
        [
            ratio_bin * (1.0 + cos_dir * cos_dir) - 0.5,
            ratio_bin * cos_dir * sin_dir,
            ratio_bin * (1.0 + sin_dir * sin_dir) - 0.5,
        ],
        0,
    ) * (4.0 / (NDIR * NFREQ))
    partial_value = jnp.dot(
        weights, energy.reshape(bin_count, cell_count), precision=lax.Precision.HIGHEST
    )
    partial_value = partial_value * ((1.0 + at_cells[2]) * sea_float.reshape(-1))
    partial_value = lax.psum(partial_value, "sect")
    contributions = jnp.concatenate([partial_value, jnp.ones((1, cell_count), jnp.float32)], 0)
    blank = jnp.zeros((tile_count * ocean_cells,), jnp.float32)
    spread = jnp.stack(
        [blank.at[target].add(contributions[k]).reshape(tile_count, -1, columns) for k in range(4)],
        1,
    )
    gathered = lax.psum_scatter(spread, "tile", scatter_dimension=0, tiled=True).reshape(4, -1)
    return (energy, gathered[:3] / jnp.maximum(gathered[3], 1.0)[None])


def solution(mesh):
    in_specs = (
        P("sect", "tile", None),
        P(),
        P(),
        P(None, "tile"),
        P("tile"),
        P("tile", None),
        P("tile", None),
        P("tile"),
    )
    out_specs = (P("sect", "tile", None), P(None, "tile"))
    return jax.shard_map(local, mesh=mesh, in_specs=in_specs, out_specs=out_specs, check_vma=False)
```

```python
import math

import jax
import jax.numpy as jnp
from jax import lax
from jax.sharding import PartitionSpec as P

NDIR = 36
NFREQ = 36
STEPS = 4


def with_halo(x, sides, width):
    for axis, dim in sides:
        size, length = (lax.axis_size(axis), x.shape[dim])
        up = [(i, (i + 1) % size) for i in range(size - 1)]
        down = [(j, i) for i, j in up]
        last = lax.slice_in_dim(x, length - width, length, axis=dim)
        leading = lax.slice_in_dim(x, 0, width, axis=dim)
        before = lax.ppermute(last, axis, up)
        after = lax.ppermute(leading, axis, down)
        x = jnp.concatenate([before, x, after], axis=dim)
    return x


def advance(energy, flow_fields, speed_x, speed_y):
    vel_x = speed_x + flow_fields[0]
    vel_y = speed_y + flow_fields[1]
    middle = energy[:, 1:-1]
    mid_vel = vel_x[:, 1:-1]
    face_x = 0.5 * (mid_vel + jnp.roll(mid_vel, -1, axis=2))
    east_side = jnp.roll(middle, -1, axis=2)
    flux_x = jnp.maximum(face_x, 0.0) * middle + jnp.minimum(face_x, 0.0) * east_side
    div_x = flux_x - jnp.roll(flux_x, 1, axis=2)
    face_y = 0.5 * (vel_y[:, :-1] + vel_y[:, 1:])
    flux_y = jnp.maximum(face_y, 0.0) * energy[:, :-1] + jnp.minimum(face_y, 0.0) * energy[:, 1:]
    div_y = flux_y[:, 1:] - flux_y[:, :-1]
    return flow_fields[2, 1:-1] * (middle - div_x - div_y)


def local(
    spectrum, courant, group_ratio, ocean_currents, elevation, sea_mask, owner_tile, ocean_slot
):
    bin_count, row_count, columns = spectrum.shape
    cell_count = row_count * columns
    tile_count = lax.axis_size("tile")
    capacity = 2 * ((cell_count + tile_count - 1) // tile_count)
    ocean_cells = elevation.shape[0]
    first_bin = lax.axis_index("sect") * bin_count
    bin_ids = first_bin + jnp.arange(bin_count, dtype=jnp.int32)
    dir_ids = bin_ids // NFREQ
    freq_ids = bin_ids % NFREQ
    freq_pick = (freq_ids[:, None] == jnp.arange(NFREQ, dtype=jnp.int32)[None, :]).astype(
        jnp.float32
    )
    group_speed = jnp.sum(freq_pick * courant[None, :], 1)
    ratio_bin = jnp.sum(freq_pick * group_ratio[None, :], 1)
    angles = (dir_ids.astype(jnp.float32) + 0.5) * (2.0 * math.pi / NDIR)
    cos_dir = jnp.cos(angles)
    sin_dir = jnp.sin(angles)
    speed_x = (group_speed * cos_dir)[:, None, None]
    speed_y = (group_speed * sin_dir)[:, None, None]
    owners = owner_tile[:, 0]
    cell_ids = jnp.arange(owners.shape[0], dtype=jnp.int32)
    same_before = (owners[None, :] == owners[:, None]) & (cell_ids[None, :] < cell_ids[:, None])
    rank_in = jnp.sum(same_before.astype(jnp.int32), 1)
    position = owners * capacity + rank_in
    requests = jnp.full((tile_count * capacity,), -1, jnp.int32).at[position].set(ocean_slot)
    asked_slots = lax.all_to_all(
        requests.reshape(tile_count, capacity), "tile", split_axis=0, concat_axis=0, tiled=True
    )
    is_valid = asked_slots >= 0
    slot_index = jnp.where(is_valid, asked_slots, 0)
    surface = jnp.concatenate([ocean_currents, elevation[None]], 0)
    answer = jnp.where(is_valid[None], surface[:, slot_index], 0.0)
    returned = lax.all_to_all(answer, "tile", split_axis=1, concat_axis=1, tiled=True)
    at_cells = returned.reshape(3, tile_count * capacity)[:, position]
    sea_float = sea_mask.astype(jnp.float32)
    flow_fields = jnp.concatenate([at_cells[:2].reshape(2, row_count, columns), sea_float[None]], 0)
    extended = with_halo(jnp.concatenate([spectrum, flow_fields], 0), (("tile", 1),), STEPS)
    energy = extended[:bin_count]
    for sub_step in range(STEPS):
        flows_now = extended[bin_count:, sub_step : extended.shape[1] - sub_step]
        energy = advance(energy, flows_now, speed_x, speed_y)
    weights = jnp.stack(
        [
            ratio_bin * (1.0 + cos_dir * cos_dir) - 0.5,
            ratio_bin * cos_dir * sin_dir,
            ratio_bin * (1.0 + sin_dir * sin_dir) - 0.5,
        ],
        0,
    ) * (4.0 / (NDIR * NFREQ))
    partial_value = jnp.dot(
        weights, energy.reshape(bin_count, cell_count), precision=lax.Precision.HIGHEST
    )
    partial_value = partial_value * ((1.0 + at_cells[2]) * sea_float.reshape(-1))
    sect_count = lax.axis_size("sect")
    every_part = lax.all_to_all(
        jnp.broadcast_to(partial_value[None], (sect_count,) + partial_value.shape),
        "sect",
        0,
        0,
        tiled=True,
    )
    partial_value = every_part[0]
    for part in range(1, sect_count):
        partial_value = partial_value + every_part[part]
    packed = jnp.zeros((3, tile_count * capacity), jnp.float32).at[:, position].set(partial_value)
    arrived = lax.all_to_all(
        packed.reshape(3, tile_count, capacity), "tile", split_axis=1, concat_axis=1, tiled=True
    )
    flat_slots = asked_slots.reshape(-1)
    weight = is_valid.reshape(-1).astype(jnp.float32)
    slot_pick = (flat_slots[:, None] == jnp.arange(ocean_cells, dtype=jnp.int32)[None, :]).astype(
        jnp.float32
    )
    summed = jnp.dot(
        jnp.concatenate([arrived.reshape(3, -1) * weight[None], weight[None]], 0),
        slot_pick,
        precision=lax.Precision.HIGHEST,
    )
    return (energy, summed[:3] / jnp.maximum(summed[3], 1.0)[None])


def solution(mesh):
    in_specs = (
        P("sect", "tile", None),
        P(),
        P(),
        P(None, "tile"),
        P("tile"),
        P("tile", None),
        P("tile", None),
        P("tile"),
    )
    out_specs = (P("sect", "tile", None), P(None, "tile"))
    return jax.shard_map(local, mesh=mesh, in_specs=in_specs, out_specs=out_specs, check_vma=False)
```

```python
import math

import jax
import jax.numpy as jnp
from jax import lax
from jax.sharding import PartitionSpec as P

NDIR = 36
NFREQ = 36
STEPS = 4


def with_halo(x, sides, width):
    for axis, dim in sides:
        size, length = (lax.axis_size(axis), x.shape[dim])
        up = [(i, (i + 1) % size) for i in range(size - 1)]
        down = [(j, i) for i, j in up]
        last = lax.slice_in_dim(x, length - width, length, axis=dim)
        leading = lax.slice_in_dim(x, 0, width, axis=dim)
        before = lax.ppermute(last, axis, up)
        after = lax.ppermute(leading, axis, down)
        x = jnp.concatenate([before, x, after], axis=dim)
    return x


def advance(energy, flow_fields, speed_x, speed_y):
    vel_x = speed_x + flow_fields[0]
    vel_y = speed_y + flow_fields[1]
    middle = energy[:, 1:-1]
    mid_vel = vel_x[:, 1:-1]
    face_x = 0.5 * (mid_vel + jnp.roll(mid_vel, -1, axis=2))
    east_side = jnp.roll(middle, -1, axis=2)
    flux_x = jnp.maximum(face_x, 0.0) * middle + jnp.minimum(face_x, 0.0) * east_side
    div_x = flux_x - jnp.roll(flux_x, 1, axis=2)
    face_y = 0.5 * (vel_y[:, :-1] + vel_y[:, 1:])
    flux_y = jnp.maximum(face_y, 0.0) * energy[:, :-1] + jnp.minimum(face_y, 0.0) * energy[:, 1:]
    div_y = flux_y[:, 1:] - flux_y[:, :-1]
    return flow_fields[2, 1:-1] * (middle - div_x - div_y)


def local(
    spectrum, courant, group_ratio, ocean_currents, elevation, sea_mask, owner_tile, ocean_slot
):
    bin_count, row_count, columns = spectrum.shape
    cell_count = row_count * columns
    tile_count = lax.axis_size("tile")
    capacity = 2 * ((cell_count + tile_count - 1) // tile_count)
    ocean_cells = elevation.shape[0]
    first_bin = lax.axis_index("sect") * bin_count
    bin_ids = first_bin + jnp.arange(bin_count, dtype=jnp.int32)
    dir_ids = bin_ids // NFREQ
    freq_ids = bin_ids % NFREQ
    freq_pick = (freq_ids[:, None] == jnp.arange(NFREQ, dtype=jnp.int32)[None, :]).astype(
        jnp.float32
    )
    group_speed = jnp.sum(freq_pick * courant[None, :], 1)
    ratio_bin = jnp.sum(freq_pick * group_ratio[None, :], 1)
    angles = (dir_ids.astype(jnp.float32) + 0.5) * (2.0 * math.pi / NDIR)
    cos_dir = jnp.cos(angles)
    sin_dir = jnp.sin(angles)
    speed_x = (group_speed * cos_dir)[:, None, None]
    speed_y = (group_speed * sin_dir)[:, None, None]
    owners = owner_tile[:, 0]
    cell_ids = jnp.arange(owners.shape[0], dtype=jnp.int32)
    same_before = (owners[None, :] == owners[:, None]) & (cell_ids[None, :] < cell_ids[:, None])
    rank_in = jnp.sum(same_before.astype(jnp.int32), 1)
    position = owners * capacity + rank_in
    spectrum_ext = with_halo(spectrum, (("tile", 1),), STEPS)
    slot_ids = jnp.arange(tile_count * capacity, dtype=jnp.int32)
    requests = (
        jnp.sum(jnp.where(position[:, None] == slot_ids[None, :], ocean_slot[:, None] + 1, 0), 0) - 1
    )
    asked_slots = lax.all_to_all(
        requests.reshape(tile_count, capacity), "tile", split_axis=0, concat_axis=0, tiled=True
    )
    is_valid = asked_slots >= 0
    slot_index = jnp.where(is_valid, asked_slots, 0)
    surface = jnp.concatenate([ocean_currents, elevation[None]], 0)
    answer = jnp.where(is_valid[None], surface[:, slot_index], 0.0)
    returned = lax.all_to_all(answer, "tile", split_axis=1, concat_axis=1, tiled=True)
    at_cells = returned.reshape(3, tile_count * capacity)[:, position]
    sea_float = sea_mask.astype(jnp.float32)
    flow_fields = jnp.concatenate([at_cells[:2].reshape(2, row_count, columns), sea_float[None]], 0)
    flows_ext = with_halo(flow_fields, (("tile", 1),), STEPS)
    energy = spectrum_ext
    for sub_step in range(STEPS):
        flows_now = flows_ext[:, sub_step : flows_ext.shape[1] - sub_step]
        energy = advance(energy, flows_now, speed_x, speed_y)
    weights = jnp.stack(
        [
            ratio_bin * (1.0 + cos_dir * cos_dir) - 0.5,
            ratio_bin * cos_dir * sin_dir,
            ratio_bin * (1.0 + sin_dir * sin_dir) - 0.5,
        ],
        0,
    ) * (4.0 / (NDIR * NFREQ))
    partial_value = jnp.dot(
        weights, energy.reshape(bin_count, cell_count), precision=lax.Precision.HIGHEST
    )
    partial_value = partial_value * ((1.0 + at_cells[2]) * sea_float.reshape(-1))
    sect_count = lax.axis_size("sect")
    every_part = lax.all_to_all(
        jnp.broadcast_to(partial_value[None], (sect_count,) + partial_value.shape),
        "sect",
        0,
        0,
        tiled=True,
    )
    partial_value = every_part[0]
    for part in range(1, sect_count):
        partial_value = partial_value + every_part[part]
    packed = jnp.zeros((3, tile_count * capacity), jnp.float32).at[:, position].set(partial_value)
    arrived = lax.all_to_all(
        packed.reshape(3, tile_count, capacity), "tile", split_axis=1, concat_axis=1, tiled=True
    )
    flat_slots = asked_slots.reshape(-1)
    weight = is_valid.reshape(-1).astype(jnp.float32)
    slot_pick = (flat_slots[:, None] == jnp.arange(ocean_cells, dtype=jnp.int32)[None, :]).astype(
        jnp.float32
    )
    summed = jnp.dot(
        jnp.concatenate([arrived.reshape(3, -1) * weight[None], weight[None]], 0),
        slot_pick,
        precision=lax.Precision.HIGHEST,
    )
    return (energy, summed[:3] / jnp.maximum(summed[3], 1.0)[None])


def solution(mesh):
    in_specs = (
        P("sect", "tile", None),
        P(),
        P(),
        P(None, "tile"),
        P("tile"),
        P("tile", None),
        P("tile", None),
        P("tile"),
    )
    out_specs = (P("sect", "tile", None), P(None, "tile"))
    return jax.shard_map(local, mesh=mesh, in_specs=in_specs, out_specs=out_specs, check_vma=False)
```

```python
import math

import jax
import jax.numpy as jnp
from jax import lax
from jax.sharding import PartitionSpec as P

NDIR = 36
NFREQ = 36
STEPS = 4


def with_halo(x, sides, width):
    for axis, dim in sides:
        size, length = (lax.axis_size(axis), x.shape[dim])
        up = [(i, (i + 1) % size) for i in range(size - 1)]
        down = [(j, i) for i, j in up]
        last = lax.slice_in_dim(x, length - width, length, axis=dim)
        leading = lax.slice_in_dim(x, 0, width, axis=dim)
        before = lax.ppermute(last, axis, up)
        after = lax.ppermute(leading, axis, down)
        x = jnp.concatenate([before, x, after], axis=dim)
    return x


def advance(energy, flow_fields, speed_x, speed_y):
    vel_x = speed_x + flow_fields[0]
    vel_y = speed_y + flow_fields[1]
    middle = energy[:, 1:-1]
    mid_vel = vel_x[:, 1:-1]
    face_x = 0.5 * (mid_vel + jnp.roll(mid_vel, -1, axis=2))
    east_side = jnp.roll(middle, -1, axis=2)
    flux_x = jnp.maximum(face_x, 0.0) * middle + jnp.minimum(face_x, 0.0) * east_side
    div_x = flux_x - jnp.roll(flux_x, 1, axis=2)
    face_y = 0.5 * (vel_y[:, :-1] + vel_y[:, 1:])
    flux_y = jnp.maximum(face_y, 0.0) * energy[:, :-1] + jnp.minimum(face_y, 0.0) * energy[:, 1:]
    div_y = flux_y[:, 1:] - flux_y[:, :-1]
    return flow_fields[2, 1:-1] * (middle - div_x - div_y)


def local(
    spectrum, courant, group_ratio, ocean_currents, elevation, sea_mask, owner_tile, ocean_slot
):
    bin_count, row_count, columns = spectrum.shape
    cell_count = row_count * columns
    tile_count = lax.axis_size("tile")
    capacity = 2 * ((cell_count + tile_count - 1) // tile_count)
    ocean_cells = elevation.shape[0]
    first_bin = lax.axis_index("sect") * bin_count
    bin_ids = first_bin + jnp.arange(bin_count, dtype=jnp.int32)
    dir_ids = bin_ids // NFREQ
    freq_ids = bin_ids % NFREQ
    freq_pick = (freq_ids[:, None] == jnp.arange(NFREQ, dtype=jnp.int32)[None, :]).astype(
        jnp.float32
    )
    group_speed = jnp.sum(freq_pick * courant[None, :], 1)
    ratio_bin = jnp.sum(freq_pick * group_ratio[None, :], 1)
    angles = (dir_ids.astype(jnp.float32) + 0.5) * (2.0 * math.pi / NDIR)
    cos_dir = jnp.cos(angles)
    sin_dir = jnp.sin(angles)
    speed_x = (group_speed * cos_dir)[:, None, None]
    speed_y = (group_speed * sin_dir)[:, None, None]
    owners = owner_tile[:, 0]
    cell_ids = jnp.arange(owners.shape[0], dtype=jnp.int32)
    same_before = (owners[None, :] == owners[:, None]) & (cell_ids[None, :] < cell_ids[:, None])
    rank_in = jnp.sum(same_before.astype(jnp.int32), 1)
    position = owners * capacity + rank_in
    slot_ids = jnp.arange(tile_count * capacity, dtype=jnp.int32)
    requests = (
        jnp.sum(jnp.where(position[:, None] == slot_ids[None, :], ocean_slot[:, None] + 1, 0), 0) - 1
    )
    asked_slots = lax.all_to_all(
        requests.reshape(tile_count, capacity), "tile", split_axis=0, concat_axis=0, tiled=True
    )
    is_valid = asked_slots >= 0
    slot_index = jnp.where(is_valid, asked_slots, 0)
    surface = jnp.concatenate([ocean_currents, elevation[None]], 0)
    answer = jnp.where(is_valid[None], surface[:, slot_index], 0.0)
    returned = lax.all_to_all(answer, "tile", split_axis=1, concat_axis=1, tiled=True)
    at_cells = returned.reshape(3, tile_count * capacity)[:, position]
    sea_float = sea_mask.astype(jnp.float32)
    flow_fields = jnp.concatenate([at_cells[:2].reshape(2, row_count, columns), sea_float[None]], 0)
    extended = with_halo(jnp.concatenate([spectrum, flow_fields], 0), (("tile", 1),), STEPS)
    energy = extended[:bin_count]
    for sub_step in range(STEPS):
        flows_now = extended[bin_count:, sub_step : extended.shape[1] - sub_step]
        energy = advance(energy, flows_now, speed_x, speed_y)
    weights = jnp.stack(
        [
            ratio_bin * (1.0 + cos_dir * cos_dir) - 0.5,
            ratio_bin * cos_dir * sin_dir,
            ratio_bin * (1.0 + sin_dir * sin_dir) - 0.5,
        ],
        0,
    ) * (4.0 / (NDIR * NFREQ))
    partial_value = jnp.dot(
        weights, energy.reshape(bin_count, cell_count), precision=lax.Precision.HIGHEST
    )
    partial_value = partial_value * ((1.0 + at_cells[2]) * sea_float.reshape(-1))
    sect_count = lax.axis_size("sect")
    every_part = lax.all_to_all(
        jnp.broadcast_to(partial_value[None], (sect_count,) + partial_value.shape),
        "sect",
        0,
        0,
        tiled=True,
    )
    partial_value = every_part[0]
    for part in range(1, sect_count):
        partial_value = partial_value + every_part[part]
    packed = jnp.zeros((3, tile_count * capacity), jnp.float32).at[:, position].set(partial_value)
    arrived = lax.all_to_all(
        packed.reshape(3, tile_count, capacity), "tile", split_axis=1, concat_axis=1, tiled=True
    )
    flat_slots = asked_slots.reshape(-1)
    weight = is_valid.reshape(-1).astype(jnp.float32)
    slot_pick = (flat_slots[:, None] == jnp.arange(ocean_cells, dtype=jnp.int32)[None, :]).astype(
        jnp.float32
    )
    summed = jnp.dot(
        jnp.concatenate([arrived.reshape(3, -1) * weight[None], weight[None]], 0),
        slot_pick,
        precision=lax.Precision.HIGHEST,
    )
    return (energy, summed[:3] / jnp.maximum(summed[3], 1.0)[None])


def solution(mesh):
    in_specs = (
        P("sect", "tile", None),
        P(),
        P(),
        P(None, "tile"),
        P("tile"),
        P("tile", None),
        P("tile", None),
        P("tile"),
    )
    out_specs = (P("sect", "tile", None), P(None, "tile"))
    return jax.shard_map(local, mesh=mesh, in_specs=in_specs, out_specs=out_specs, check_vma=False)
```

```python
import functools
import math

import jax
import jax.numpy as jnp
from jax import lax
from jax.experimental import pallas as pl
from jax.experimental.pallas import tpu as pltpu
from jax.sharding import PartitionSpec as P

NDIR = 36
NFREQ = 36
STEPS = 4


def with_halo(x, sides, width):
    for axis, dim in sides:
        size, length = (lax.axis_size(axis), x.shape[dim])
        up = [(i, (i + 1) % size) for i in range(size - 1)]
        down = [(j, i) for i, j in up]
        last = lax.slice_in_dim(x, length - width, length, axis=dim)
        leading = lax.slice_in_dim(x, 0, width, axis=dim)
        before = lax.ppermute(last, axis, up)
        after = lax.ppermute(leading, axis, down)
        x = jnp.concatenate([before, x, after], axis=dim)
    return x


def advance(energy, flow_fields, speed_x, speed_y):
    vel_x = speed_x + flow_fields[0]
    vel_y = speed_y + flow_fields[1]
    middle = energy[:, 1:-1]
    mid_vel = vel_x[:, 1:-1]
    face_x = 0.5 * (mid_vel + jnp.roll(mid_vel, -1, axis=2))
    east_side = jnp.roll(middle, -1, axis=2)
    flux_x = jnp.maximum(face_x, 0.0) * middle + jnp.minimum(face_x, 0.0) * east_side
    div_x = flux_x - jnp.roll(flux_x, 1, axis=2)
    face_y = 0.5 * (vel_y[:, :-1] + vel_y[:, 1:])
    flux_y = jnp.maximum(face_y, 0.0) * energy[:, :-1] + jnp.minimum(face_y, 0.0) * energy[:, 1:]
    div_y = flux_y[:, 1:] - flux_y[:, :-1]
    return flow_fields[2, 1:-1] * (middle - div_x - div_y)


def propagate_kernel(speed_ref, energy_ref, flow_ref, out_ref, *, block, steps, rows_out):
    rows = energy_ref.shape[1]
    lanes = energy_ref.shape[2]
    base = pl.program_id(0) * block
    u = flow_ref[0]
    v = flow_ref[1]
    m = flow_ref[2]

    def one_bin(b, carry):
        vel_x = speed_ref[0, base + b] + u
        vel_y = speed_ref[1, base + b] + v
        face_x = 0.5 * (vel_x + pltpu.roll(vel_x, lanes - 1, 1))
        face_y = 0.5 * (vel_y + pltpu.roll(vel_y, rows - 1, 0))
        pos_x = jnp.maximum(face_x, 0.0)
        neg_x = jnp.minimum(face_x, 0.0)
        pos_y = jnp.maximum(face_y, 0.0)
        neg_y = jnp.minimum(face_y, 0.0)
        energy = energy_ref[b]
        for _ in range(steps):
            flux_x = pos_x * energy + neg_x * pltpu.roll(energy, lanes - 1, 1)
            div_x = flux_x - pltpu.roll(flux_x, 1, 1)
            flux_y = pos_y * energy + neg_y * pltpu.roll(energy, rows - 1, 0)
            div_y = flux_y - pltpu.roll(flux_y, 1, 0)
            energy = m * (energy - div_x - div_y)
        out_ref[b] = pltpu.roll(energy, rows - steps, 0)[:rows_out]
        return carry

    lax.fori_loop(0, block, one_bin, 0)


def propagate(speeds, extended, bins, rows_out):
    rows, lanes = extended.shape[1:]
    block = max(d for d in range(1, 33) if bins % d == 0)
    kernel = functools.partial(propagate_kernel, block=block, steps=STEPS, rows_out=rows_out)
    return pl.pallas_call(
        kernel,
        grid=(bins // block,),
        in_specs=[
            pl.BlockSpec(memory_space=pltpu.MemorySpace.SMEM),
            pl.BlockSpec((block, rows, lanes), lambda i: (i, 0, 0)),
            pl.BlockSpec((3, rows, lanes), lambda i: (bins // 3, 0, 0)),
        ],
        out_specs=pl.BlockSpec((block, rows_out, lanes), lambda i: (i, 0, 0)),
        out_shape=jax.ShapeDtypeStruct((bins, rows_out, lanes), jnp.float32),
    )(speeds, extended, extended)


def local(
    spectrum, courant, group_ratio, ocean_currents, elevation, sea_mask, owner_tile, ocean_slot
):
    bin_count, row_count, columns = spectrum.shape
    cell_count = row_count * columns
    tile_count = lax.axis_size("tile")
    capacity = 2 * ((cell_count + tile_count - 1) // tile_count)
    ocean_cells = elevation.shape[0]
    first_bin = lax.axis_index("sect") * bin_count
    bin_ids = first_bin + jnp.arange(bin_count, dtype=jnp.int32)
    dir_ids = bin_ids // NFREQ
    freq_ids = bin_ids % NFREQ
    freq_pick = (freq_ids[:, None] == jnp.arange(NFREQ, dtype=jnp.int32)[None, :]).astype(
        jnp.float32
    )
    group_speed = jnp.sum(freq_pick * courant[None, :], 1)
    ratio_bin = jnp.sum(freq_pick * group_ratio[None, :], 1)
    angles = (dir_ids.astype(jnp.float32) + 0.5) * (2.0 * math.pi / NDIR)
    cos_dir = jnp.cos(angles)
    sin_dir = jnp.sin(angles)
    owners = owner_tile[:, 0]
    cell_ids = jnp.arange(owners.shape[0], dtype=jnp.int32)
    same_before = (owners[None, :] == owners[:, None]) & (cell_ids[None, :] < cell_ids[:, None])
    rank_in = jnp.sum(same_before.astype(jnp.int32), 1)
    position = owners * capacity + rank_in
    slot_ids = jnp.arange(tile_count * capacity, dtype=jnp.int32)
    requests = (
        jnp.sum(jnp.where(position[:, None] == slot_ids[None, :], ocean_slot[:, None] + 1, 0), 0) - 1
    )
    asked_slots = lax.all_to_all(
        requests.reshape(tile_count, capacity), "tile", split_axis=0, concat_axis=0, tiled=True
    )
    is_valid = asked_slots >= 0
    slot_index = jnp.where(is_valid, asked_slots, 0)
    surface = jnp.concatenate([ocean_currents, elevation[None]], 0)
    answer = jnp.where(is_valid[None], surface[:, slot_index], 0.0)
    returned = lax.all_to_all(answer, "tile", split_axis=1, concat_axis=1, tiled=True)
    at_cells = returned.reshape(3, tile_count * capacity)[:, position]
    sea_float = sea_mask.astype(jnp.float32)
    flow_fields = jnp.concatenate([at_cells[:2].reshape(2, row_count, columns), sea_float[None]], 0)
    extended = with_halo(jnp.concatenate([spectrum, flow_fields], 0), (("tile", 1),), STEPS)
    speeds = jnp.stack([group_speed * cos_dir, group_speed * sin_dir], 0)
    energy = propagate(speeds, extended, bin_count, row_count)
    weights = jnp.stack(
        [
            ratio_bin * (1.0 + cos_dir * cos_dir) - 0.5,
            ratio_bin * cos_dir * sin_dir,
            ratio_bin * (1.0 + sin_dir * sin_dir) - 0.5,
        ],
        0,
    ) * (4.0 / (NDIR * NFREQ))
    partial_value = jnp.dot(
        weights, energy.reshape(bin_count, cell_count), precision=lax.Precision.HIGHEST
    )
    partial_value = partial_value * ((1.0 + at_cells[2]) * sea_float.reshape(-1))
    sect_count = lax.axis_size("sect")
    every_part = lax.all_to_all(
        jnp.broadcast_to(partial_value[None], (sect_count,) + partial_value.shape),
        "sect",
        0,
        0,
        tiled=True,
    )
    partial_value = every_part[0]
    for part in range(1, sect_count):
        partial_value = partial_value + every_part[part]
    packed = jnp.zeros((3, tile_count * capacity), jnp.float32).at[:, position].set(partial_value)
    arrived = lax.all_to_all(
        packed.reshape(3, tile_count, capacity), "tile", split_axis=1, concat_axis=1, tiled=True
    )
    flat_slots = asked_slots.reshape(-1)
    weight = is_valid.reshape(-1).astype(jnp.float32)
    slot_pick = (flat_slots[:, None] == jnp.arange(ocean_cells, dtype=jnp.int32)[None, :]).astype(
        jnp.float32
    )
    summed = jnp.dot(
        jnp.concatenate([arrived.reshape(3, -1) * weight[None], weight[None]], 0),
        slot_pick,
        precision=lax.Precision.HIGHEST,
    )
    return (energy, summed[:3] / jnp.maximum(summed[3], 1.0)[None])


def solution(mesh):
    in_specs = (
        P("sect", "tile", None),
        P(),
        P(),
        P(None, "tile"),
        P("tile"),
        P("tile", None),
        P("tile", None),
        P("tile"),
    )
    out_specs = (P("sect", "tile", None), P(None, "tile"))
    return jax.shard_map(local, mesh=mesh, in_specs=in_specs, out_specs=out_specs, check_vma=False)
```

```python
import functools
import math

import jax
import jax.numpy as jnp
from jax import lax
from jax.experimental import pallas as pl
from jax.experimental.pallas import tpu as pltpu
from jax.sharding import PartitionSpec as P

NDIR = 36
NFREQ = 36
STEPS = 4


def with_halo(x, sides, width):
    for axis, dim in sides:
        size, length = (lax.axis_size(axis), x.shape[dim])
        up = [(i, (i + 1) % size) for i in range(size - 1)]
        down = [(j, i) for i, j in up]
        last = lax.slice_in_dim(x, length - width, length, axis=dim)
        leading = lax.slice_in_dim(x, 0, width, axis=dim)
        before = lax.ppermute(last, axis, up)
        after = lax.ppermute(leading, axis, down)
        x = jnp.concatenate([before, x, after], axis=dim)
    return x


def advance(energy, flow_fields, speed_x, speed_y):
    vel_x = speed_x + flow_fields[0]
    vel_y = speed_y + flow_fields[1]
    middle = energy[:, 1:-1]
    mid_vel = vel_x[:, 1:-1]
    face_x = 0.5 * (mid_vel + jnp.roll(mid_vel, -1, axis=2))
    east_side = jnp.roll(middle, -1, axis=2)
    flux_x = jnp.maximum(face_x, 0.0) * middle + jnp.minimum(face_x, 0.0) * east_side
    div_x = flux_x - jnp.roll(flux_x, 1, axis=2)
    face_y = 0.5 * (vel_y[:, :-1] + vel_y[:, 1:])
    flux_y = jnp.maximum(face_y, 0.0) * energy[:, :-1] + jnp.minimum(face_y, 0.0) * energy[:, 1:]
    div_y = flux_y[:, 1:] - flux_y[:, :-1]
    return flow_fields[2, 1:-1] * (middle - div_x - div_y)


def propagate_kernel(speed_ref, energy_ref, flow_ref, out_ref, *, block, steps, rows_out):
    rows = energy_ref.shape[1]
    lanes = energy_ref.shape[2]
    base = pl.program_id(0) * block
    u = flow_ref[0]
    v = flow_ref[1]
    m = flow_ref[2]

    def one_bin(b, carry):
        vel_x = speed_ref[0, base + b] + u
        vel_y = speed_ref[1, base + b] + v
        face_x = 0.5 * (vel_x + pltpu.roll(vel_x, lanes - 1, 1))
        face_y = 0.5 * (vel_y + pltpu.roll(vel_y, rows - 1, 0))
        pos_x = jnp.maximum(face_x, 0.0)
        neg_x = jnp.minimum(face_x, 0.0)
        pos_y = jnp.maximum(face_y, 0.0)
        neg_y = jnp.minimum(face_y, 0.0)
        energy = energy_ref[b]
        for _ in range(steps):
            flux_x = pos_x * energy + neg_x * pltpu.roll(energy, lanes - 1, 1)
            div_x = flux_x - pltpu.roll(flux_x, 1, 1)
            flux_y = pos_y * energy + neg_y * pltpu.roll(energy, rows - 1, 0)
            div_y = flux_y - pltpu.roll(flux_y, 1, 0)
            energy = m * (energy - div_x - div_y)
        out_ref[b] = pltpu.roll(energy, rows - steps, 0)[:rows_out]
        return carry

    lax.fori_loop(0, block, one_bin, 0, unroll=True)


def propagate(speeds, extended, bins, rows_out):
    rows, lanes = extended.shape[1:]
    block = max(d for d in range(1, 33) if bins % d == 0)
    kernel = functools.partial(propagate_kernel, block=block, steps=STEPS, rows_out=rows_out)
    return pl.pallas_call(
        kernel,
        grid=(bins // block,),
        in_specs=[
            pl.BlockSpec(memory_space=pltpu.MemorySpace.SMEM),
            pl.BlockSpec((block, rows, lanes), lambda i: (i, 0, 0)),
            pl.BlockSpec((3, rows, lanes), lambda i: (bins // 3, 0, 0)),
        ],
        out_specs=pl.BlockSpec((block, rows_out, lanes), lambda i: (i, 0, 0)),
        out_shape=jax.ShapeDtypeStruct((bins, rows_out, lanes), jnp.float32),
    )(speeds, extended, extended)


def local(
    spectrum, courant, group_ratio, ocean_currents, elevation, sea_mask, owner_tile, ocean_slot
):
    bin_count, row_count, columns = spectrum.shape
    cell_count = row_count * columns
    tile_count = lax.axis_size("tile")
    capacity = 2 * ((cell_count + tile_count - 1) // tile_count)
    ocean_cells = elevation.shape[0]
    first_bin = lax.axis_index("sect") * bin_count
    bin_ids = first_bin + jnp.arange(bin_count, dtype=jnp.int32)
    dir_ids = bin_ids // NFREQ
    freq_ids = bin_ids % NFREQ
    freq_pick = (freq_ids[:, None] == jnp.arange(NFREQ, dtype=jnp.int32)[None, :]).astype(
        jnp.float32
    )
    group_speed = jnp.sum(freq_pick * courant[None, :], 1)
    ratio_bin = jnp.sum(freq_pick * group_ratio[None, :], 1)
    angles = (dir_ids.astype(jnp.float32) + 0.5) * (2.0 * math.pi / NDIR)
    cos_dir = jnp.cos(angles)
    sin_dir = jnp.sin(angles)
    owners = owner_tile[:, 0]
    cell_ids = jnp.arange(owners.shape[0], dtype=jnp.int32)
    same_before = (owners[None, :] == owners[:, None]) & (cell_ids[None, :] < cell_ids[:, None])
    rank_in = jnp.sum(same_before.astype(jnp.int32), 1)
    position = owners * capacity + rank_in
    slot_ids = jnp.arange(tile_count * capacity, dtype=jnp.int32)
    requests = (
        jnp.sum(jnp.where(position[:, None] == slot_ids[None, :], ocean_slot[:, None] + 1, 0), 0) - 1
    )
    asked_slots = lax.all_to_all(
        requests.reshape(tile_count, capacity), "tile", split_axis=0, concat_axis=0, tiled=True
    )
    is_valid = asked_slots >= 0
    slot_index = jnp.where(is_valid, asked_slots, 0)
    surface = jnp.concatenate([ocean_currents, elevation[None]], 0)
    answer = jnp.where(is_valid[None], surface[:, slot_index], 0.0)
    returned = lax.all_to_all(answer, "tile", split_axis=1, concat_axis=1, tiled=True)
    at_cells = returned.reshape(3, tile_count * capacity)[:, position]
    sea_float = sea_mask.astype(jnp.float32)
    flow_fields = jnp.concatenate([at_cells[:2].reshape(2, row_count, columns), sea_float[None]], 0)
    extended = with_halo(jnp.concatenate([spectrum, flow_fields], 0), (("tile", 1),), STEPS)
    speeds = jnp.stack([group_speed * cos_dir, group_speed * sin_dir], 0)
    energy = propagate(speeds, extended, bin_count, row_count)
    weights = jnp.stack(
        [
            ratio_bin * (1.0 + cos_dir * cos_dir) - 0.5,
            ratio_bin * cos_dir * sin_dir,
            ratio_bin * (1.0 + sin_dir * sin_dir) - 0.5,
        ],
        0,
    ) * (4.0 / (NDIR * NFREQ))
    partial_value = jnp.dot(
        weights, energy.reshape(bin_count, cell_count), precision=lax.Precision.HIGHEST
    )
    partial_value = partial_value * ((1.0 + at_cells[2]) * sea_float.reshape(-1))
    sect_count = lax.axis_size("sect")
    every_part = lax.all_to_all(
        jnp.broadcast_to(partial_value[None], (sect_count,) + partial_value.shape),
        "sect",
        0,
        0,
        tiled=True,
    )
    partial_value = every_part[0]
    for part in range(1, sect_count):
        partial_value = partial_value + every_part[part]
    packed = jnp.zeros((3, tile_count * capacity), jnp.float32).at[:, position].set(partial_value)
    arrived = lax.all_to_all(
        packed.reshape(3, tile_count, capacity), "tile", split_axis=1, concat_axis=1, tiled=True
    )
    flat_slots = asked_slots.reshape(-1)
    weight = is_valid.reshape(-1).astype(jnp.float32)
    slot_pick = (flat_slots[:, None] == jnp.arange(ocean_cells, dtype=jnp.int32)[None, :]).astype(
        jnp.float32
    )
    summed = jnp.dot(
        jnp.concatenate([arrived.reshape(3, -1) * weight[None], weight[None]], 0),
        slot_pick,
        precision=lax.Precision.HIGHEST,
    )
    return (energy, summed[:3] / jnp.maximum(summed[3], 1.0)[None])


def solution(mesh):
    in_specs = (
        P("sect", "tile", None),
        P(),
        P(),
        P(None, "tile"),
        P("tile"),
        P("tile", None),
        P("tile", None),
        P("tile"),
    )
    out_specs = (P("sect", "tile", None), P(None, "tile"))
    return jax.shard_map(local, mesh=mesh, in_specs=in_specs, out_specs=out_specs, check_vma=False)
```

```python
import functools
import math

import jax
import jax.numpy as jnp
from jax import lax
from jax.experimental import pallas as pl
from jax.experimental.pallas import tpu as pltpu
from jax.sharding import PartitionSpec as P

NDIR = 36
NFREQ = 36
STEPS = 4


def with_halo(x, sides, width):
    for axis, dim in sides:
        size, length = (lax.axis_size(axis), x.shape[dim])
        up = [(i, (i + 1) % size) for i in range(size - 1)]
        down = [(j, i) for i, j in up]
        last = lax.slice_in_dim(x, length - width, length, axis=dim)
        leading = lax.slice_in_dim(x, 0, width, axis=dim)
        before = lax.ppermute(last, axis, up)
        after = lax.ppermute(leading, axis, down)
        x = jnp.concatenate([before, x, after], axis=dim)
    return x


def advance(energy, flow_fields, speed_x, speed_y):
    vel_x = speed_x + flow_fields[0]
    vel_y = speed_y + flow_fields[1]
    middle = energy[:, 1:-1]
    mid_vel = vel_x[:, 1:-1]
    face_x = 0.5 * (mid_vel + jnp.roll(mid_vel, -1, axis=2))
    east_side = jnp.roll(middle, -1, axis=2)
    flux_x = jnp.maximum(face_x, 0.0) * middle + jnp.minimum(face_x, 0.0) * east_side
    div_x = flux_x - jnp.roll(flux_x, 1, axis=2)
    face_y = 0.5 * (vel_y[:, :-1] + vel_y[:, 1:])
    flux_y = jnp.maximum(face_y, 0.0) * energy[:, :-1] + jnp.minimum(face_y, 0.0) * energy[:, 1:]
    div_y = flux_y[:, 1:] - flux_y[:, :-1]
    return flow_fields[2, 1:-1] * (middle - div_x - div_y)


def propagate_kernel(speed_ref, energy_ref, flow_ref, out_ref, *, block, steps, rows_out):
    rows = energy_ref.shape[1]
    lanes = energy_ref.shape[2]
    base = pl.program_id(0) * block
    u = flow_ref[0]
    v = flow_ref[1]
    m = flow_ref[2]

    def one_bin(b, carry):
        vel_x = speed_ref[0, base + b] + u
        vel_y = speed_ref[1, base + b] + v
        face_x = 0.5 * (vel_x + pltpu.roll(vel_x, lanes - 1, 1))
        face_y = 0.5 * (vel_y + pltpu.roll(vel_y, rows - 1, 0))
        pos_x = jnp.maximum(face_x, 0.0)
        neg_x = jnp.minimum(face_x, 0.0)
        pos_y = jnp.maximum(face_y, 0.0)
        neg_y = jnp.minimum(face_y, 0.0)
        energy = energy_ref[b]
        for _ in range(steps):
            flux_x = pos_x * energy + neg_x * pltpu.roll(energy, lanes - 1, 1)
            div_x = flux_x - pltpu.roll(flux_x, 1, 1)
            flux_y = pos_y * energy + neg_y * pltpu.roll(energy, rows - 1, 0)
            div_y = flux_y - pltpu.roll(flux_y, 1, 0)
            energy = m * (energy - div_x - div_y)
        out_ref[b] = pltpu.roll(energy, rows - steps, 0)[:rows_out]
        return carry

    lax.fori_loop(0, block, one_bin, 0, unroll=True)


def propagate(speeds, extended, bins, rows_out):
    rows, lanes = extended.shape[1:]
    block = max(d for d in range(1, 33) if bins % d == 0)
    kernel = functools.partial(propagate_kernel, block=block, steps=STEPS, rows_out=rows_out)
    return pl.pallas_call(
        kernel,
        grid=(bins // block,),
        in_specs=[
            pl.BlockSpec(memory_space=pltpu.MemorySpace.SMEM),
            pl.BlockSpec((block, rows, lanes), lambda i: (i, 0, 0)),
            pl.BlockSpec((3, rows, lanes), lambda i: (bins // 3, 0, 0)),
        ],
        out_specs=pl.BlockSpec((block, rows_out, lanes), lambda i: (i, 0, 0)),
        out_shape=jax.ShapeDtypeStruct((bins, rows_out, lanes), jnp.float32),
    )(speeds, extended, extended)


def local(
    spectrum, courant, group_ratio, ocean_currents, elevation, sea_mask, owner_tile, ocean_slot
):
    bin_count, row_count, columns = spectrum.shape
    cell_count = row_count * columns
    tile_count = lax.axis_size("tile")
    capacity = 2 * ((cell_count + tile_count - 1) // tile_count)
    ocean_cells = elevation.shape[0]
    first_bin = lax.axis_index("sect") * bin_count
    bin_ids = first_bin + jnp.arange(bin_count, dtype=jnp.int32)
    dir_ids = bin_ids // NFREQ
    freq_ids = bin_ids % NFREQ
    freq_pick = (freq_ids[:, None] == jnp.arange(NFREQ, dtype=jnp.int32)[None, :]).astype(
        jnp.float32
    )
    group_speed = jnp.sum(freq_pick * courant[None, :], 1)
    ratio_bin = jnp.sum(freq_pick * group_ratio[None, :], 1)
    angles = (dir_ids.astype(jnp.float32) + 0.5) * (2.0 * math.pi / NDIR)
    cos_dir = jnp.cos(angles)
    sin_dir = jnp.sin(angles)
    owners = owner_tile[:, 0]
    cell_ids = jnp.arange(owners.shape[0], dtype=jnp.int32)
    same_before = (owners[None, :] == owners[:, None]) & (cell_ids[None, :] < cell_ids[:, None])
    rank_in = jnp.sum(same_before.astype(jnp.int32), 1)
    position = owners * capacity + rank_in
    slot_ids = jnp.arange(tile_count * capacity, dtype=jnp.int32)
    requests = (
        jnp.sum(jnp.where(position[:, None] == slot_ids[None, :], ocean_slot[:, None] + 1, 0), 0) - 1
    )
    asked_slots = lax.all_to_all(
        requests.reshape(tile_count, capacity), "tile", split_axis=0, concat_axis=0, tiled=True
    )
    is_valid = asked_slots >= 0
    slot_index = jnp.where(is_valid, asked_slots, 0)
    surface = jnp.concatenate([ocean_currents, elevation[None]], 0)
    asked_pick = (
        asked_slots.reshape(-1)[:, None] == jnp.arange(ocean_cells, dtype=jnp.int32)[None, :]
    ).astype(jnp.float32)
    answer = lax.optimization_barrier(
        jnp.dot(asked_pick, surface.T, precision=lax.Precision.HIGHEST)
    ).T.reshape(
        3, tile_count, capacity
    )
    returned = lax.all_to_all(answer, "tile", split_axis=1, concat_axis=1, tiled=True)
    cell_pick = (position[:, None] == slot_ids[None, :]).astype(jnp.float32)
    at_cells = lax.optimization_barrier(
        jnp.dot(
            cell_pick, returned.reshape(3, tile_count * capacity).T, precision=lax.Precision.HIGHEST
        )
    ).T
    sea_float = sea_mask.astype(jnp.float32)
    flow_fields = jnp.concatenate([at_cells[:2].reshape(2, row_count, columns), sea_float[None]], 0)
    extended = with_halo(jnp.concatenate([spectrum, flow_fields], 0), (("tile", 1),), STEPS)
    speeds = jnp.stack([group_speed * cos_dir, group_speed * sin_dir], 0)
    energy = propagate(speeds, extended, bin_count, row_count)
    weights = jnp.stack(
        [
            ratio_bin * (1.0 + cos_dir * cos_dir) - 0.5,
            ratio_bin * cos_dir * sin_dir,
            ratio_bin * (1.0 + sin_dir * sin_dir) - 0.5,
        ],
        0,
    ) * (4.0 / (NDIR * NFREQ))
    partial_value = jnp.dot(
        weights, energy.reshape(bin_count, cell_count), precision=lax.Precision.HIGHEST
    )
    partial_value = partial_value * ((1.0 + at_cells[2]) * sea_float.reshape(-1))
    sect_count = lax.axis_size("sect")
    every_part = lax.all_to_all(
        jnp.broadcast_to(partial_value[None], (sect_count,) + partial_value.shape),
        "sect",
        0,
        0,
        tiled=True,
    )
    partial_value = every_part[0]
    for part in range(1, sect_count):
        partial_value = partial_value + every_part[part]
    packed = jnp.zeros((3, tile_count * capacity), jnp.float32).at[:, position].set(partial_value)
    arrived = lax.all_to_all(
        packed.reshape(3, tile_count, capacity), "tile", split_axis=1, concat_axis=1, tiled=True
    )
    flat_slots = asked_slots.reshape(-1)
    weight = is_valid.reshape(-1).astype(jnp.float32)
    slot_pick = (jnp.arange(ocean_cells, dtype=jnp.int32)[:, None] == flat_slots[None, :]).astype(
        jnp.float32
    )
    summed = lax.optimization_barrier(
        jnp.dot(
            slot_pick,
            jnp.concatenate([arrived.reshape(3, -1) * weight[None], weight[None]], 0).T,
            precision=lax.Precision.HIGHEST,
        )
    ).T
    return (energy, summed[:3] / jnp.maximum(summed[3], 1.0)[None])


def solution(mesh):
    in_specs = (
        P("sect", "tile", None),
        P(),
        P(),
        P(None, "tile"),
        P("tile"),
        P("tile", None),
        P("tile", None),
        P("tile"),
    )
    out_specs = (P("sect", "tile", None), P(None, "tile"))
    return jax.shard_map(local, mesh=mesh, in_specs=in_specs, out_specs=out_specs, check_vma=False)
```

```python
import functools
import math

import jax
import jax.numpy as jnp
from jax import lax
from jax.experimental import pallas as pl
from jax.experimental.pallas import tpu as pltpu
from jax.sharding import PartitionSpec as P

NDIR = 36
NFREQ = 36
STEPS = 4


def with_halo(x, sides, width):
    for axis, dim in sides:
        size, length = (lax.axis_size(axis), x.shape[dim])
        up = [(i, (i + 1) % size) for i in range(size - 1)]
        down = [(j, i) for i, j in up]
        last = lax.slice_in_dim(x, length - width, length, axis=dim)
        leading = lax.slice_in_dim(x, 0, width, axis=dim)
        before = lax.ppermute(last, axis, up)
        after = lax.ppermute(leading, axis, down)
        x = jnp.concatenate([before, x, after], axis=dim)
    return x


def advance(energy, flow_fields, speed_x, speed_y):
    vel_x = speed_x + flow_fields[0]
    vel_y = speed_y + flow_fields[1]
    middle = energy[:, 1:-1]
    mid_vel = vel_x[:, 1:-1]
    face_x = 0.5 * (mid_vel + jnp.roll(mid_vel, -1, axis=2))
    east_side = jnp.roll(middle, -1, axis=2)
    flux_x = jnp.maximum(face_x, 0.0) * middle + jnp.minimum(face_x, 0.0) * east_side
    div_x = flux_x - jnp.roll(flux_x, 1, axis=2)
    face_y = 0.5 * (vel_y[:, :-1] + vel_y[:, 1:])
    flux_y = jnp.maximum(face_y, 0.0) * energy[:, :-1] + jnp.minimum(face_y, 0.0) * energy[:, 1:]
    div_y = flux_y[:, 1:] - flux_y[:, :-1]
    return flow_fields[2, 1:-1] * (middle - div_x - div_y)


def propagate_kernel(
    speed_ref, weight_ref, energy_ref, flow_ref, out_ref, stress_ref, *, block, steps, rows_out
):
    rows = energy_ref.shape[1]
    lanes = energy_ref.shape[2]
    base = pl.program_id(0) * block
    u = flow_ref[0]
    v = flow_ref[1]
    m = flow_ref[2]

    @pl.when(pl.program_id(0) == 0)
    def _():
        stress_ref[...] = jnp.zeros(stress_ref.shape, jnp.float32)

    def one_bin(b, carry):
        vel_x = speed_ref[0, base + b] + u
        vel_y = speed_ref[1, base + b] + v
        face_x = 0.5 * (vel_x + pltpu.roll(vel_x, lanes - 1, 1))
        face_y = 0.5 * (vel_y + pltpu.roll(vel_y, rows - 1, 0))
        pos_x = jnp.maximum(face_x, 0.0)
        neg_x = jnp.minimum(face_x, 0.0)
        pos_y = jnp.maximum(face_y, 0.0)
        neg_y = jnp.minimum(face_y, 0.0)
        energy = energy_ref[b]
        for _ in range(steps):
            flux_x = pos_x * energy + neg_x * pltpu.roll(energy, lanes - 1, 1)
            div_x = flux_x - pltpu.roll(flux_x, 1, 1)
            flux_y = pos_y * energy + neg_y * pltpu.roll(energy, rows - 1, 0)
            div_y = flux_y - pltpu.roll(flux_y, 1, 0)
            energy = m * (energy - div_x - div_y)
        kept = pltpu.roll(energy, rows - steps, 0)[:rows_out]
        out_ref[b] = kept
        return tuple(carry[k] + weight_ref[k, base + b] * kept for k in range(3))

    zero = jnp.zeros((rows_out, lanes), jnp.float32)
    sums = lax.fori_loop(0, block, one_bin, (zero, zero, zero), unroll=True)
    for k in range(3):
        stress_ref[k] = stress_ref[k] + sums[k]


def propagate(speeds, weights, extended, bins, rows_out):
    rows, lanes = extended.shape[1:]
    block = max(d for d in range(1, 33) if bins % d == 0)
    kernel = functools.partial(propagate_kernel, block=block, steps=STEPS, rows_out=rows_out)
    return pl.pallas_call(
        kernel,
        grid=(bins // block,),
        in_specs=[
            pl.BlockSpec(memory_space=pltpu.MemorySpace.SMEM),
            pl.BlockSpec(memory_space=pltpu.MemorySpace.SMEM),
            pl.BlockSpec((block, rows, lanes), lambda i: (i, 0, 0)),
            pl.BlockSpec((3, rows, lanes), lambda i: (bins // 3, 0, 0)),
        ],
        out_specs=[
            pl.BlockSpec((block, rows_out, lanes), lambda i: (i, 0, 0)),
            pl.BlockSpec((3, rows_out, lanes), lambda i: (0, 0, 0)),
        ],
        out_shape=[
            jax.ShapeDtypeStruct((bins, rows_out, lanes), jnp.float32),
            jax.ShapeDtypeStruct((3, rows_out, lanes), jnp.float32),
        ],
    )(speeds, weights, extended, extended)

def local(
    spectrum, courant, group_ratio, ocean_currents, elevation, sea_mask, owner_tile, ocean_slot
):
    bin_count, row_count, columns = spectrum.shape
    cell_count = row_count * columns
    tile_count = lax.axis_size("tile")
    capacity = 2 * ((cell_count + tile_count - 1) // tile_count)
    ocean_cells = elevation.shape[0]
    first_bin = lax.axis_index("sect") * bin_count
    bin_ids = first_bin + jnp.arange(bin_count, dtype=jnp.int32)
    dir_ids = bin_ids // NFREQ
    freq_ids = bin_ids % NFREQ
    freq_pick = (freq_ids[:, None] == jnp.arange(NFREQ, dtype=jnp.int32)[None, :]).astype(
        jnp.float32
    )
    group_speed = jnp.sum(freq_pick * courant[None, :], 1)
    ratio_bin = jnp.sum(freq_pick * group_ratio[None, :], 1)
    angles = (dir_ids.astype(jnp.float32) + 0.5) * (2.0 * math.pi / NDIR)
    cos_dir = jnp.cos(angles)
    sin_dir = jnp.sin(angles)
    owners = owner_tile[:, 0]
    cell_ids = jnp.arange(owners.shape[0], dtype=jnp.int32)
    same_before = (owners[None, :] == owners[:, None]) & (cell_ids[None, :] < cell_ids[:, None])
    rank_in = jnp.sum(same_before.astype(jnp.int32), 1)
    position = owners * capacity + rank_in
    slot_ids = jnp.arange(tile_count * capacity, dtype=jnp.int32)
    requests = (
        jnp.sum(jnp.where(position[:, None] == slot_ids[None, :], ocean_slot[:, None] + 1, 0), 0) - 1
    )
    asked_slots = lax.all_to_all(
        requests.reshape(tile_count, capacity), "tile", split_axis=0, concat_axis=0, tiled=True
    )
    is_valid = asked_slots >= 0
    slot_index = jnp.where(is_valid, asked_slots, 0)
    surface = jnp.concatenate([ocean_currents, elevation[None]], 0)
    answer = jnp.where(is_valid[None], surface[:, slot_index], 0.0)
    returned = lax.all_to_all(answer, "tile", split_axis=1, concat_axis=1, tiled=True)
    at_cells = returned.reshape(3, tile_count * capacity)[:, position]
    sea_float = sea_mask.astype(jnp.float32)
    flow_fields = jnp.concatenate([at_cells[:2].reshape(2, row_count, columns), sea_float[None]], 0)
    extended = with_halo(jnp.concatenate([spectrum, flow_fields], 0), (("tile", 1),), STEPS)
    speeds = jnp.stack([group_speed * cos_dir, group_speed * sin_dir], 0)
    weights = jnp.stack(
        [
            ratio_bin * (1.0 + cos_dir * cos_dir) - 0.5,
            ratio_bin * cos_dir * sin_dir,
            ratio_bin * (1.0 + sin_dir * sin_dir) - 0.5,
        ],
        0,
    ) * (4.0 / (NDIR * NFREQ))
    energy, partial_value = propagate(speeds, weights, extended, bin_count, row_count)
    partial_value = partial_value.reshape(3, cell_count)
    partial_value = partial_value * ((1.0 + at_cells[2]) * sea_float.reshape(-1))
    sect_count = lax.axis_size("sect")
    every_part = lax.all_to_all(
        jnp.broadcast_to(partial_value[None], (sect_count,) + partial_value.shape),
        "sect",
        0,
        0,
        tiled=True,
    )
    partial_value = every_part[0]
    for part in range(1, sect_count):
        partial_value = partial_value + every_part[part]
    packed = jnp.zeros((3, tile_count * capacity), jnp.float32).at[:, position].set(partial_value)
    arrived = lax.all_to_all(
        packed.reshape(3, tile_count, capacity), "tile", split_axis=1, concat_axis=1, tiled=True
    )
    flat_slots = asked_slots.reshape(-1)
    weight = is_valid.reshape(-1).astype(jnp.float32)
    slot_pick = (flat_slots[:, None] == jnp.arange(ocean_cells, dtype=jnp.int32)[None, :]).astype(
        jnp.float32
    )
    summed = jnp.dot(
        jnp.concatenate([arrived.reshape(3, -1) * weight[None], weight[None]], 0),
        slot_pick,
        precision=lax.Precision.HIGHEST,
    )
    return (energy, summed[:3] / jnp.maximum(summed[3], 1.0)[None])


def solution(mesh):
    in_specs = (
        P("sect", "tile", None),
        P(),
        P(),
        P(None, "tile"),
        P("tile"),
        P("tile", None),
        P("tile", None),
        P("tile"),
    )
    out_specs = (P("sect", "tile", None), P(None, "tile"))
    return jax.shard_map(local, mesh=mesh, in_specs=in_specs, out_specs=out_specs, check_vma=False)
```

```python
import functools
import math

import jax
import jax.numpy as jnp
from jax import lax
from jax.experimental import pallas as pl
from jax.experimental.pallas import tpu as pltpu
from jax.sharding import PartitionSpec as P

NDIR = 36
NFREQ = 36
STEPS = 4


def with_halo(x, sides, width):
    for axis, dim in sides:
        size, length = (lax.axis_size(axis), x.shape[dim])
        up = [(i, (i + 1) % size) for i in range(size - 1)]
        down = [(j, i) for i, j in up]
        last = lax.slice_in_dim(x, length - width, length, axis=dim)
        leading = lax.slice_in_dim(x, 0, width, axis=dim)
        before = lax.ppermute(last, axis, up)
        after = lax.ppermute(leading, axis, down)
        x = jnp.concatenate([before, x, after], axis=dim)
    return x


def advance(energy, flow_fields, speed_x, speed_y):
    vel_x = speed_x + flow_fields[0]
    vel_y = speed_y + flow_fields[1]
    middle = energy[:, 1:-1]
    mid_vel = vel_x[:, 1:-1]
    face_x = 0.5 * (mid_vel + jnp.roll(mid_vel, -1, axis=2))
    east_side = jnp.roll(middle, -1, axis=2)
    flux_x = jnp.maximum(face_x, 0.0) * middle + jnp.minimum(face_x, 0.0) * east_side
    div_x = flux_x - jnp.roll(flux_x, 1, axis=2)
    face_y = 0.5 * (vel_y[:, :-1] + vel_y[:, 1:])
    flux_y = jnp.maximum(face_y, 0.0) * energy[:, :-1] + jnp.minimum(face_y, 0.0) * energy[:, 1:]
    div_y = flux_y[:, 1:] - flux_y[:, :-1]
    return flow_fields[2, 1:-1] * (middle - div_x - div_y)


def propagate_kernel(
    speed_ref, weight_ref, energy_ref, flow_ref, out_ref, stress_ref, *, block, steps, rows_out
):
    rows = energy_ref.shape[1]
    lanes = energy_ref.shape[2]
    base = pl.program_id(0) * block
    u = flow_ref[0]
    v = flow_ref[1]
    m = flow_ref[2]

    @pl.when(pl.program_id(0) == 0)
    def _():
        stress_ref[...] = jnp.zeros(stress_ref.shape, jnp.float32)

    def one_bin(b, carry):
        vel_x = speed_ref[0, base + b] + u
        vel_y = speed_ref[1, base + b] + v
        face_x = 0.5 * (vel_x + pltpu.roll(vel_x, lanes - 1, 1))
        face_y = 0.5 * (vel_y + pltpu.roll(vel_y, rows - 1, 0))
        pos_x = jnp.maximum(face_x, 0.0)
        neg_x = jnp.minimum(face_x, 0.0)
        pos_y = jnp.maximum(face_y, 0.0)
        neg_y = jnp.minimum(face_y, 0.0)
        energy = energy_ref[b]
        for _ in range(steps):
            flux_x = pos_x * energy + neg_x * pltpu.roll(energy, lanes - 1, 1)
            div_x = flux_x - pltpu.roll(flux_x, 1, 1)
            flux_y = pos_y * energy + neg_y * pltpu.roll(energy, rows - 1, 0)
            div_y = flux_y - pltpu.roll(flux_y, 1, 0)
            energy = m * (energy - div_x - div_y)
        kept = pltpu.roll(energy, rows - steps, 0)[:rows_out]
        out_ref[b] = kept
        return tuple(carry[k] + weight_ref[k, base + b] * kept for k in range(3))

    zero = jnp.zeros((rows_out, lanes), jnp.float32)
    sums = lax.fori_loop(0, block, one_bin, (zero, zero, zero), unroll=True)
    for k in range(3):
        stress_ref[k] = stress_ref[k] + sums[k]


def propagate(speeds, weights, extended, bins, rows_out):
    rows, lanes = extended.shape[1:]
    block = max(d for d in range(1, 33) if bins % d == 0)
    kernel = functools.partial(propagate_kernel, block=block, steps=STEPS, rows_out=rows_out)
    return pl.pallas_call(
        kernel,
        grid=(bins // block,),
        in_specs=[
            pl.BlockSpec(memory_space=pltpu.MemorySpace.SMEM),
            pl.BlockSpec(memory_space=pltpu.MemorySpace.SMEM),
            pl.BlockSpec((block, rows, lanes), lambda i: (i, 0, 0)),
            pl.BlockSpec((3, rows, lanes), lambda i: (bins // 3, 0, 0)),
        ],
        out_specs=[
            pl.BlockSpec((block, rows_out, lanes), lambda i: (i, 0, 0)),
            pl.BlockSpec((3, rows_out, lanes), lambda i: (0, 0, 0)),
        ],
        out_shape=[
            jax.ShapeDtypeStruct((bins, rows_out, lanes), jnp.float32),
            jax.ShapeDtypeStruct((3, rows_out, lanes), jnp.float32),
        ],
    )(speeds, weights, extended, extended)

def pick_matmul(values, pick):
    parts = []
    rest = values
    for _ in range(2):
        head = lax.reduce_precision(rest, exponent_bits=8, mantissa_bits=7)
        parts.append(head)
        rest = rest - head
    parts.append(rest)
    rows = values.shape[0]
    stacked = jnp.concatenate(parts, 0).astype(jnp.bfloat16)
    product = jnp.dot(stacked, pick, preferred_element_type=jnp.float32)
    return (product[:rows] + product[rows : 2 * rows]) + product[2 * rows :]


def local(
    spectrum, courant, group_ratio, ocean_currents, elevation, sea_mask, owner_tile, ocean_slot
):
    bin_count, row_count, columns = spectrum.shape
    cell_count = row_count * columns
    tile_count = lax.axis_size("tile")
    capacity = 2 * ((cell_count + tile_count - 1) // tile_count)
    ocean_cells = elevation.shape[0]
    first_bin = lax.axis_index("sect") * bin_count
    bin_ids = first_bin + jnp.arange(bin_count, dtype=jnp.int32)
    dir_ids = bin_ids // NFREQ
    freq_ids = bin_ids % NFREQ
    freq_pick = (freq_ids[:, None] == jnp.arange(NFREQ, dtype=jnp.int32)[None, :]).astype(
        jnp.float32
    )
    group_speed = jnp.sum(freq_pick * courant[None, :], 1)
    ratio_bin = jnp.sum(freq_pick * group_ratio[None, :], 1)
    angles = (dir_ids.astype(jnp.float32) + 0.5) * (2.0 * math.pi / NDIR)
    cos_dir = jnp.cos(angles)
    sin_dir = jnp.sin(angles)
    owners = owner_tile[:, 0]
    cell_ids = jnp.arange(owners.shape[0], dtype=jnp.int32)
    same_before = (owners[None, :] == owners[:, None]) & (cell_ids[None, :] < cell_ids[:, None])
    rank_in = jnp.sum(same_before.astype(jnp.int32), 1)
    position = owners * capacity + rank_in
    slot_ids = jnp.arange(tile_count * capacity, dtype=jnp.int32)
    requests = (
        jnp.sum(jnp.where(position[:, None] == slot_ids[None, :], ocean_slot[:, None] + 1, 0), 0) - 1
    )
    asked_slots = lax.all_to_all(
        requests.reshape(tile_count, capacity), "tile", split_axis=0, concat_axis=0, tiled=True
    )
    is_valid = asked_slots >= 0
    slot_index = jnp.where(is_valid, asked_slots, 0)
    surface = jnp.concatenate([ocean_currents, elevation[None]], 0)
    ocean_ids = jnp.arange(ocean_cells, dtype=jnp.int32)
    slot_pick = (ocean_ids[:, None] == asked_slots.reshape(-1)[None, :]).astype(jnp.bfloat16)
    answer = pick_matmul(surface, slot_pick).reshape(3, tile_count, capacity)
    returned = lax.all_to_all(answer, "tile", split_axis=1, concat_axis=1, tiled=True)
    cell_pick = (slot_ids[:, None] == position[None, :]).astype(jnp.bfloat16)
    at_cells = pick_matmul(returned.reshape(3, tile_count * capacity), cell_pick)
    sea_float = sea_mask.astype(jnp.float32)
    flow_fields = jnp.concatenate([at_cells[:2].reshape(2, row_count, columns), sea_float[None]], 0)
    extended = with_halo(jnp.concatenate([spectrum, flow_fields], 0), (("tile", 1),), STEPS)
    speeds = jnp.stack([group_speed * cos_dir, group_speed * sin_dir], 0)
    weights = jnp.stack(
        [
            ratio_bin * (1.0 + cos_dir * cos_dir) - 0.5,
            ratio_bin * cos_dir * sin_dir,
            ratio_bin * (1.0 + sin_dir * sin_dir) - 0.5,
        ],
        0,
    ) * (4.0 / (NDIR * NFREQ))
    energy, partial_value = propagate(speeds, weights, extended, bin_count, row_count)
    partial_value = partial_value.reshape(3, cell_count)
    partial_value = partial_value * ((1.0 + at_cells[2]) * sea_float.reshape(-1))
    sect_count = lax.axis_size("sect")
    every_part = lax.all_to_all(
        jnp.broadcast_to(partial_value[None], (sect_count,) + partial_value.shape),
        "sect",
        0,
        0,
        tiled=True,
    )
    partial_value = every_part[0]
    for part in range(1, sect_count):
        partial_value = partial_value + every_part[part]
    packed = jnp.zeros((3, tile_count * capacity), jnp.float32).at[:, position].set(partial_value)
    arrived = lax.all_to_all(
        packed.reshape(3, tile_count, capacity), "tile", split_axis=1, concat_axis=1, tiled=True
    )
    flat_slots = asked_slots.reshape(-1)
    weight = is_valid.reshape(-1).astype(jnp.float32)
    summed = pick_matmul(
        jnp.concatenate([arrived.reshape(3, -1) * weight[None], weight[None]], 0), slot_pick.T
    )
    return (energy, summed[:3] / jnp.maximum(summed[3], 1.0)[None])


def solution(mesh):
    in_specs = (
        P("sect", "tile", None),
        P(),
        P(),
        P(None, "tile"),
        P("tile"),
        P("tile", None),
        P("tile", None),
        P("tile"),
    )
    out_specs = (P("sect", "tile", None), P(None, "tile"))
    return jax.shard_map(local, mesh=mesh, in_specs=in_specs, out_specs=out_specs, check_vma=False)
```

```python
import functools
import math

import jax
import jax.numpy as jnp
from jax import lax
from jax.experimental import pallas as pl
from jax.experimental.pallas import tpu as pltpu
from jax.sharding import PartitionSpec as P

NDIR = 36
NFREQ = 36
STEPS = 4


def with_halo(x, sides, width):
    for axis, dim in sides:
        size, length = (lax.axis_size(axis), x.shape[dim])
        up = [(i, (i + 1) % size) for i in range(size - 1)]
        down = [(j, i) for i, j in up]
        last = lax.slice_in_dim(x, length - width, length, axis=dim)
        leading = lax.slice_in_dim(x, 0, width, axis=dim)
        before = lax.ppermute(last, axis, up)
        after = lax.ppermute(leading, axis, down)
        x = jnp.concatenate([before, x, after], axis=dim)
    return x


def advance(energy, flow_fields, speed_x, speed_y):
    vel_x = speed_x + flow_fields[0]
    vel_y = speed_y + flow_fields[1]
    middle = energy[:, 1:-1]
    mid_vel = vel_x[:, 1:-1]
    face_x = 0.5 * (mid_vel + jnp.roll(mid_vel, -1, axis=2))
    east_side = jnp.roll(middle, -1, axis=2)
    flux_x = jnp.maximum(face_x, 0.0) * middle + jnp.minimum(face_x, 0.0) * east_side
    div_x = flux_x - jnp.roll(flux_x, 1, axis=2)
    face_y = 0.5 * (vel_y[:, :-1] + vel_y[:, 1:])
    flux_y = jnp.maximum(face_y, 0.0) * energy[:, :-1] + jnp.minimum(face_y, 0.0) * energy[:, 1:]
    div_y = flux_y[:, 1:] - flux_y[:, :-1]
    return flow_fields[2, 1:-1] * (middle - div_x - div_y)


def propagate_kernel(
    speed_ref, weight_ref, energy_ref, flow_ref, out_ref, stress_ref, *, block, steps, rows_out
):
    rows = energy_ref.shape[1]
    lanes = energy_ref.shape[2]
    base = pl.program_id(0) * block
    u = flow_ref[0]
    v = flow_ref[1]
    m = flow_ref[2]

    @pl.when(pl.program_id(0) == 0)
    def _():
        stress_ref[...] = jnp.zeros(stress_ref.shape, jnp.float32)

    def one_bin(b, carry):
        vel_x = speed_ref[0, base + b] + u
        vel_y = speed_ref[1, base + b] + v
        face_x = 0.5 * (vel_x + pltpu.roll(vel_x, lanes - 1, 1))
        face_y = 0.5 * (vel_y + pltpu.roll(vel_y, rows - 1, 0))
        pos_x = jnp.maximum(face_x, 0.0)
        neg_x = jnp.minimum(face_x, 0.0)
        pos_y = jnp.maximum(face_y, 0.0)
        neg_y = jnp.minimum(face_y, 0.0)
        energy = energy_ref[b]
        for _ in range(steps):
            flux_x = pos_x * energy + neg_x * pltpu.roll(energy, lanes - 1, 1)
            div_x = flux_x - pltpu.roll(flux_x, 1, 1)
            flux_y = pos_y * energy + neg_y * pltpu.roll(energy, rows - 1, 0)
            div_y = flux_y - pltpu.roll(flux_y, 1, 0)
            energy = m * (energy - div_x - div_y)
        kept = pltpu.roll(energy, rows - steps, 0)[:rows_out]
        out_ref[b] = kept
        return tuple(carry[k] + weight_ref[k, base + b] * kept for k in range(3))

    zero = jnp.zeros((rows_out, lanes), jnp.float32)
    sums = lax.fori_loop(0, block, one_bin, (zero, zero, zero), unroll=True)
    for k in range(3):
        stress_ref[k] = stress_ref[k] + sums[k]


def propagate(speeds, weights, extended, bins, rows_out):
    rows, lanes = extended.shape[1:]
    block = max(d for d in range(1, 33) if bins % d == 0)
    kernel = functools.partial(propagate_kernel, block=block, steps=STEPS, rows_out=rows_out)
    return pl.pallas_call(
        kernel,
        grid=(bins // block,),
        in_specs=[
            pl.BlockSpec(memory_space=pltpu.MemorySpace.SMEM),
            pl.BlockSpec(memory_space=pltpu.MemorySpace.SMEM),
            pl.BlockSpec((block, rows, lanes), lambda i: (i, 0, 0)),
            pl.BlockSpec((3, rows, lanes), lambda i: (bins // 3, 0, 0)),
        ],
        out_specs=[
            pl.BlockSpec((block, rows_out, lanes), lambda i: (i, 0, 0)),
            pl.BlockSpec((3, rows_out, lanes), lambda i: (0, 0, 0)),
        ],
        out_shape=[
            jax.ShapeDtypeStruct((bins, rows_out, lanes), jnp.float32),
            jax.ShapeDtypeStruct((3, rows_out, lanes), jnp.float32),
        ],
    )(speeds, weights, extended, extended)

def pick_matmul(values, pick):
    parts = []
    rest = values
    for _ in range(2):
        head = lax.reduce_precision(rest, exponent_bits=8, mantissa_bits=7)
        parts.append(head)
        rest = rest - head
    parts.append(rest)
    rows = values.shape[0]
    stacked = jnp.concatenate(parts, 0).astype(jnp.bfloat16)
    product = jnp.dot(stacked, pick, preferred_element_type=jnp.float32)
    return (product[:rows] + product[rows : 2 * rows]) + product[2 * rows :]


def local(
    spectrum, courant, group_ratio, ocean_currents, elevation, sea_mask, owner_tile, ocean_slot
):
    bin_count, row_count, columns = spectrum.shape
    cell_count = row_count * columns
    tile_count = lax.axis_size("tile")
    capacity = 2 * ((cell_count + tile_count - 1) // tile_count)
    ocean_cells = elevation.shape[0]
    first_bin = lax.axis_index("sect") * bin_count
    bin_ids = first_bin + jnp.arange(bin_count, dtype=jnp.int32)
    dir_ids = bin_ids // NFREQ
    freq_ids = bin_ids % NFREQ
    freq_pick = (freq_ids[:, None] == jnp.arange(NFREQ, dtype=jnp.int32)[None, :]).astype(
        jnp.float32
    )
    group_speed = jnp.sum(freq_pick * courant[None, :], 1)
    ratio_bin = jnp.sum(freq_pick * group_ratio[None, :], 1)
    angles = (dir_ids.astype(jnp.float32) + 0.5) * (2.0 * math.pi / NDIR)
    cos_dir = jnp.cos(angles)
    sin_dir = jnp.sin(angles)
    owners = owner_tile[:, 0]
    cell_ids = jnp.arange(owners.shape[0], dtype=jnp.int32)
    same_before = (owners[None, :] == owners[:, None]) & (cell_ids[None, :] < cell_ids[:, None])
    rank_in = jnp.sum(same_before.astype(jnp.int32), 1)
    position = owners * capacity + rank_in
    slot_ids = jnp.arange(tile_count * capacity, dtype=jnp.int32)
    requests = (
        jnp.sum(jnp.where(position[:, None] == slot_ids[None, :], ocean_slot[:, None] + 1, 0), 0) - 1
    )
    asked_slots = lax.all_to_all(
        requests.reshape(tile_count, capacity), "tile", split_axis=0, concat_axis=0, tiled=True
    )
    is_valid = asked_slots >= 0
    surface = jnp.concatenate([ocean_currents, elevation[None]], 0)
    ocean_ids = jnp.arange(ocean_cells, dtype=jnp.int32)
    slot_pick = (ocean_ids[:, None] == asked_slots.reshape(-1)[None, :]).astype(jnp.bfloat16)
    answer = pick_matmul(surface, slot_pick).reshape(3, tile_count, capacity)
    returned = lax.all_to_all(answer, "tile", split_axis=1, concat_axis=1, tiled=True)
    cell_pick = (slot_ids[:, None] == position[None, :]).astype(jnp.bfloat16)
    at_cells = pick_matmul(returned.reshape(3, tile_count * capacity), cell_pick)
    sea_float = sea_mask.astype(jnp.float32)
    flow_fields = jnp.concatenate([at_cells[:2].reshape(2, row_count, columns), sea_float[None]], 0)
    extended = with_halo(jnp.concatenate([spectrum, flow_fields], 0), (("tile", 1),), STEPS)
    speeds = jnp.stack([group_speed * cos_dir, group_speed * sin_dir], 0)
    weights = jnp.stack(
        [
            ratio_bin * (1.0 + cos_dir * cos_dir) - 0.5,
            ratio_bin * cos_dir * sin_dir,
            ratio_bin * (1.0 + sin_dir * sin_dir) - 0.5,
        ],
        0,
    ) * (4.0 / (NDIR * NFREQ))
    energy, partial_value = propagate(speeds, weights, extended, bin_count, row_count)
    partial_value = partial_value.reshape(3, cell_count)
    partial_value = partial_value * ((1.0 + at_cells[2]) * sea_float.reshape(-1))
    sect_count = lax.axis_size("sect")
    every_part = lax.all_to_all(
        jnp.broadcast_to(partial_value[None], (sect_count,) + partial_value.shape),
        "sect",
        0,
        0,
        tiled=True,
    )
    partial_value = every_part[0]
    for part in range(1, sect_count):
        partial_value = partial_value + every_part[part]
    packed = pick_matmul(partial_value, cell_pick.T)
    arrived = lax.all_to_all(
        packed.reshape(3, tile_count, capacity), "tile", split_axis=1, concat_axis=1, tiled=True
    )
    weight = is_valid.reshape(-1).astype(jnp.float32)
    summed = pick_matmul(
        jnp.concatenate([arrived.reshape(3, -1) * weight[None], weight[None]], 0), slot_pick.T
    )
    return (energy, summed[:3] / jnp.maximum(summed[3], 1.0)[None])


def solution(mesh):
    in_specs = (
        P("sect", "tile", None),
        P(),
        P(),
        P(None, "tile"),
        P("tile"),
        P("tile", None),
        P("tile", None),
        P("tile"),
    )
    out_specs = (P("sect", "tile", None), P(None, "tile"))
    return jax.shard_map(local, mesh=mesh, in_specs=in_specs, out_specs=out_specs, check_vma=False)
```

```python
import functools
import math

import jax
import jax.numpy as jnp
from jax import lax
from jax.experimental import pallas as pl
from jax.experimental.pallas import tpu as pltpu
from jax.sharding import PartitionSpec as P

NDIR = 36
NFREQ = 36
STEPS = 4


def with_halo(x, sides, width):
    for axis, dim in sides:
        size, length = (lax.axis_size(axis), x.shape[dim])
        up = [(i, (i + 1) % size) for i in range(size - 1)]
        down = [(j, i) for i, j in up]
        last = lax.slice_in_dim(x, length - width, length, axis=dim)
        leading = lax.slice_in_dim(x, 0, width, axis=dim)
        before = lax.ppermute(last, axis, up)
        after = lax.ppermute(leading, axis, down)
        x = jnp.concatenate([before, x, after], axis=dim)
    return x


def advance(energy, flow_fields, speed_x, speed_y):
    vel_x = speed_x + flow_fields[0]
    vel_y = speed_y + flow_fields[1]
    middle = energy[:, 1:-1]
    mid_vel = vel_x[:, 1:-1]
    face_x = 0.5 * (mid_vel + jnp.roll(mid_vel, -1, axis=2))
    east_side = jnp.roll(middle, -1, axis=2)
    flux_x = jnp.maximum(face_x, 0.0) * middle + jnp.minimum(face_x, 0.0) * east_side
    div_x = flux_x - jnp.roll(flux_x, 1, axis=2)
    face_y = 0.5 * (vel_y[:, :-1] + vel_y[:, 1:])
    flux_y = jnp.maximum(face_y, 0.0) * energy[:, :-1] + jnp.minimum(face_y, 0.0) * energy[:, 1:]
    div_y = flux_y[:, 1:] - flux_y[:, :-1]
    return flow_fields[2, 1:-1] * (middle - div_x - div_y)


def propagate_kernel(
    speed_ref, weight_ref, energy_ref, flow_ref, out_ref, stress_ref, *, block, steps, rows_out
):
    rows = energy_ref.shape[1]
    lanes = energy_ref.shape[2]
    base = pl.program_id(0) * block
    u = flow_ref[0]
    v = flow_ref[1]
    m = flow_ref[2]

    @pl.when(pl.program_id(0) == 0)
    def _():
        stress_ref[...] = jnp.zeros(stress_ref.shape, jnp.float32)

    def one_bin(b, carry):
        vel_x = speed_ref[0, base + b] + u
        vel_y = speed_ref[1, base + b] + v
        face_x = 0.5 * (vel_x + pltpu.roll(vel_x, lanes - 1, 1))
        face_y = 0.5 * (vel_y + pltpu.roll(vel_y, rows - 1, 0))
        pos_x = jnp.maximum(face_x, 0.0)
        neg_x = jnp.minimum(face_x, 0.0)
        pos_y = jnp.maximum(face_y, 0.0)
        neg_y = jnp.minimum(face_y, 0.0)
        energy = energy_ref[b]
        for _ in range(steps):
            flux_x = pos_x * energy + neg_x * pltpu.roll(energy, lanes - 1, 1)
            div_x = flux_x - pltpu.roll(flux_x, 1, 1)
            flux_y = pos_y * energy + neg_y * pltpu.roll(energy, rows - 1, 0)
            div_y = flux_y - pltpu.roll(flux_y, 1, 0)
            energy = m * (energy - div_x - div_y)
        kept = pltpu.roll(energy, rows - steps, 0)[:rows_out]
        out_ref[b] = kept
        return tuple(carry[k] + weight_ref[k, base + b] * kept for k in range(3))

    zero = jnp.zeros((rows_out, lanes), jnp.float32)
    sums = lax.fori_loop(0, block, one_bin, (zero, zero, zero), unroll=True)
    for k in range(3):
        stress_ref[k] = stress_ref[k] + sums[k]


def propagate(speeds, weights, extended, bins, rows_out):
    rows, lanes = extended.shape[1:]
    block = max(d for d in range(1, 33) if bins % d == 0)
    kernel = functools.partial(propagate_kernel, block=block, steps=STEPS, rows_out=rows_out)
    return pl.pallas_call(
        kernel,
        grid=(bins // block,),
        in_specs=[
            pl.BlockSpec(memory_space=pltpu.MemorySpace.SMEM),
            pl.BlockSpec(memory_space=pltpu.MemorySpace.SMEM),
            pl.BlockSpec((block, rows, lanes), lambda i: (i, 0, 0)),
            pl.BlockSpec((3, rows, lanes), lambda i: (bins // 3, 0, 0)),
        ],
        out_specs=[
            pl.BlockSpec((block, rows_out, lanes), lambda i: (i, 0, 0)),
            pl.BlockSpec((3, rows_out, lanes), lambda i: (0, 0, 0)),
        ],
        out_shape=[
            jax.ShapeDtypeStruct((bins, rows_out, lanes), jnp.float32),
            jax.ShapeDtypeStruct((3, rows_out, lanes), jnp.float32),
        ],
    )(speeds, weights, extended, extended)

def pick_matmul(values, pick):
    parts = []
    rest = values
    for _ in range(2):
        head = lax.reduce_precision(rest, exponent_bits=8, mantissa_bits=7)
        parts.append(head)
        rest = rest - head
    parts.append(rest)
    rows = values.shape[0]
    stacked = jnp.concatenate(parts, 0).astype(jnp.bfloat16)
    product = jnp.dot(stacked, pick, preferred_element_type=jnp.float32)
    return (product[:rows] + product[rows : 2 * rows]) + product[2 * rows :]


def local(
    spectrum, courant, group_ratio, ocean_currents, elevation, sea_mask, owner_tile, ocean_slot
):
    bin_count, row_count, columns = spectrum.shape
    cell_count = row_count * columns
    tile_count = lax.axis_size("tile")
    capacity = 2 * ((cell_count + tile_count - 1) // tile_count)
    ocean_cells = elevation.shape[0]
    first_bin = lax.axis_index("sect") * bin_count
    bin_ids = first_bin + jnp.arange(bin_count, dtype=jnp.int32)
    dir_ids = bin_ids // NFREQ
    freq_ids = bin_ids % NFREQ
    freq_pick = (freq_ids[:, None] == jnp.arange(NFREQ, dtype=jnp.int32)[None, :]).astype(
        jnp.float32
    )
    group_speed = jnp.sum(freq_pick * courant[None, :], 1)
    ratio_bin = jnp.sum(freq_pick * group_ratio[None, :], 1)
    angles = (dir_ids.astype(jnp.float32) + 0.5) * (2.0 * math.pi / NDIR)
    cos_dir = jnp.cos(angles)
    sin_dir = jnp.sin(angles)
    owners = owner_tile[:, 0]
    cell_ids = jnp.arange(owners.shape[0], dtype=jnp.int32)
    same_before = (owners[None, :] == owners[:, None]) & (cell_ids[None, :] < cell_ids[:, None])
    rank_in = jnp.sum(same_before.astype(jnp.int32), 1)
    position = owners * capacity + rank_in
    slot_ids = jnp.arange(tile_count * capacity, dtype=jnp.int32)
    cell_pick = (slot_ids[:, None] == position[None, :]).astype(jnp.bfloat16)
    wanted = pick_matmul((ocean_slot + 1).astype(jnp.float32)[None], cell_pick.T)
    requests = jnp.round(wanted[0]).astype(jnp.int32) - 1
    asked_slots = lax.all_to_all(
        requests.reshape(tile_count, capacity), "tile", split_axis=0, concat_axis=0, tiled=True
    )
    is_valid = asked_slots >= 0
    surface = jnp.concatenate([ocean_currents, elevation[None]], 0)
    ocean_ids = jnp.arange(ocean_cells, dtype=jnp.int32)
    slot_pick = (ocean_ids[:, None] == asked_slots.reshape(-1)[None, :]).astype(jnp.bfloat16)
    answer = pick_matmul(surface, slot_pick).reshape(3, tile_count, capacity)
    returned = lax.all_to_all(answer, "tile", split_axis=1, concat_axis=1, tiled=True)
    at_cells = pick_matmul(returned.reshape(3, tile_count * capacity), cell_pick)
    sea_float = sea_mask.astype(jnp.float32)
    flow_fields = jnp.concatenate([at_cells[:2].reshape(2, row_count, columns), sea_float[None]], 0)
    extended = with_halo(jnp.concatenate([spectrum, flow_fields], 0), (("tile", 1),), STEPS)
    speeds = jnp.stack([group_speed * cos_dir, group_speed * sin_dir], 0)
    weights = jnp.stack(
        [
            ratio_bin * (1.0 + cos_dir * cos_dir) - 0.5,
            ratio_bin * cos_dir * sin_dir,
            ratio_bin * (1.0 + sin_dir * sin_dir) - 0.5,
        ],
        0,
    ) * (4.0 / (NDIR * NFREQ))
    energy, partial_value = propagate(speeds, weights, extended, bin_count, row_count)
    partial_value = partial_value.reshape(3, cell_count)
    partial_value = partial_value * ((1.0 + at_cells[2]) * sea_float.reshape(-1))
    sect_count = lax.axis_size("sect")
    every_part = lax.all_to_all(
        jnp.broadcast_to(partial_value[None], (sect_count,) + partial_value.shape),
        "sect",
        0,
        0,
        tiled=True,
    )
    partial_value = every_part[0]
    for part in range(1, sect_count):
        partial_value = partial_value + every_part[part]
    packed = pick_matmul(partial_value, cell_pick.T)
    arrived = lax.all_to_all(
        packed.reshape(3, tile_count, capacity), "tile", split_axis=1, concat_axis=1, tiled=True
    )
    weight = is_valid.reshape(-1).astype(jnp.float32)
    summed = pick_matmul(
        jnp.concatenate([arrived.reshape(3, -1) * weight[None], weight[None]], 0), slot_pick.T
    )
    return (energy, summed[:3] / jnp.maximum(summed[3], 1.0)[None])


def solution(mesh):
    in_specs = (
        P("sect", "tile", None),
        P(),
        P(),
        P(None, "tile"),
        P("tile"),
        P("tile", None),
        P("tile", None),
        P("tile"),
    )
    out_specs = (P("sect", "tile", None), P(None, "tile"))
    return jax.shard_map(local, mesh=mesh, in_specs=in_specs, out_specs=out_specs, check_vma=False)
```

```python
import functools
import math

import jax
import jax.numpy as jnp
from jax import lax
from jax.experimental import pallas as pl
from jax.experimental.pallas import tpu as pltpu
from jax.sharding import PartitionSpec as P

NDIR = 36
NFREQ = 36
STEPS = 4


def with_halo(x, sides, width):
    for axis, dim in sides:
        size, length = (lax.axis_size(axis), x.shape[dim])
        up = [(i, (i + 1) % size) for i in range(size - 1)]
        down = [(j, i) for i, j in up]
        last = lax.slice_in_dim(x, length - width, length, axis=dim)
        leading = lax.slice_in_dim(x, 0, width, axis=dim)
        before = lax.ppermute(last, axis, up)
        after = lax.ppermute(leading, axis, down)
        x = jnp.concatenate([before, x, after], axis=dim)
    return x


def advance(energy, flow_fields, speed_x, speed_y):
    vel_x = speed_x + flow_fields[0]
    vel_y = speed_y + flow_fields[1]
    middle = energy[:, 1:-1]
    mid_vel = vel_x[:, 1:-1]
    face_x = 0.5 * (mid_vel + jnp.roll(mid_vel, -1, axis=2))
    east_side = jnp.roll(middle, -1, axis=2)
    flux_x = jnp.maximum(face_x, 0.0) * middle + jnp.minimum(face_x, 0.0) * east_side
    div_x = flux_x - jnp.roll(flux_x, 1, axis=2)
    face_y = 0.5 * (vel_y[:, :-1] + vel_y[:, 1:])
    flux_y = jnp.maximum(face_y, 0.0) * energy[:, :-1] + jnp.minimum(face_y, 0.0) * energy[:, 1:]
    div_y = flux_y[:, 1:] - flux_y[:, :-1]
    return flow_fields[2, 1:-1] * (middle - div_x - div_y)


def propagate_kernel(
    speed_ref,
    weight_ref,
    energy_ref,
    flow_ref,
    before_ref,
    after_ref,
    flow_before_ref,
    flow_after_ref,
    factor_ref,
    out_ref,
    stress_ref,
    window_ref,
    flow_window_ref,
    *,
    block,
    steps,
):
    rows_out = energy_ref.shape[1]
    width = before_ref.shape[1]
    rows = rows_out + 2 * width
    lanes = energy_ref.shape[2]
    base = pl.program_id(0) * block

    @pl.when(pl.program_id(0) == 0)
    def _():
        stress_ref[...] = jnp.zeros(stress_ref.shape, jnp.float32)

    flow_window_ref[:, :rows_out] = flow_ref[...]
    flow_window_ref[:, rows_out : rows_out + width] = flow_after_ref[...]
    flow_window_ref[:, rows_out + width :] = flow_before_ref[...]
    u = flow_window_ref[0]
    v = flow_window_ref[1]
    m = flow_window_ref[2]

    def one_bin(b, carry):
        window_ref[b, :rows_out] = energy_ref[b]
        window_ref[b, rows_out : rows_out + width] = after_ref[b]
        window_ref[b, rows_out + width :] = before_ref[b]
        vel_x = speed_ref[0, base + b] + u
        vel_y = speed_ref[1, base + b] + v
        face_x = 0.5 * (vel_x + pltpu.roll(vel_x, lanes - 1, 1))
        face_y = 0.5 * (vel_y + pltpu.roll(vel_y, rows - 1, 0))
        pos_x = jnp.maximum(face_x, 0.0)
        neg_x = jnp.minimum(face_x, 0.0)
        pos_y = jnp.maximum(face_y, 0.0)
        neg_y = jnp.minimum(face_y, 0.0)
        energy = window_ref[b]
        for _ in range(steps):
            flux_x = pos_x * energy + neg_x * pltpu.roll(energy, lanes - 1, 1)
            div_x = flux_x - pltpu.roll(flux_x, 1, 1)
            flux_y = pos_y * energy + neg_y * pltpu.roll(energy, rows - 1, 0)
            div_y = flux_y - pltpu.roll(flux_y, 1, 0)
            energy = m * (energy - div_x - div_y)
        kept = energy[:rows_out]
        out_ref[b] = kept
        return tuple(carry[k] + weight_ref[k, base + b] * kept for k in range(3))

    zero = jnp.zeros((rows_out, lanes), jnp.float32)
    sums = lax.fori_loop(0, block, one_bin, (zero, zero, zero), unroll=True)
    for k in range(3):
        stress_ref[k] = stress_ref[k] + sums[k]

    @pl.when(pl.program_id(0) == pl.num_programs(0) - 1)
    def _():
        for k in range(3):
            stress_ref[k] = stress_ref[k] * factor_ref[...]


def propagate(speeds, weights, spectrum, flow_fields, before, after, factor):
    bins, rows_out, lanes = spectrum.shape
    width = before.shape[1]
    block = max(d for d in range(1, 33) if bins % d == 0)
    kernel = functools.partial(propagate_kernel, block=block, steps=STEPS)
    flows_at = bins // 3
    return pl.pallas_call(
        kernel,
        grid=(bins // block,),
        in_specs=[
            pl.BlockSpec(memory_space=pltpu.MemorySpace.SMEM),
            pl.BlockSpec(memory_space=pltpu.MemorySpace.SMEM),
            pl.BlockSpec((block, rows_out, lanes), lambda i: (i, 0, 0)),
            pl.BlockSpec((3, rows_out, lanes), lambda i: (0, 0, 0)),
            pl.BlockSpec((block, width, lanes), lambda i: (i, 0, 0)),
            pl.BlockSpec((block, width, lanes), lambda i: (i, 0, 0)),
            pl.BlockSpec((3, width, lanes), lambda i: (flows_at, 0, 0)),
            pl.BlockSpec((3, width, lanes), lambda i: (flows_at, 0, 0)),
            pl.BlockSpec((rows_out, lanes), lambda i: (0, 0)),
        ],
        out_specs=[
            pl.BlockSpec((block, rows_out, lanes), lambda i: (i, 0, 0)),
            pl.BlockSpec((3, rows_out, lanes), lambda i: (0, 0, 0)),
        ],
        out_shape=[
            jax.ShapeDtypeStruct((bins, rows_out, lanes), jnp.float32),
            jax.ShapeDtypeStruct((3, rows_out, lanes), jnp.float32),
        ],
        scratch_shapes=[
            pltpu.VMEM((block, rows_out + 2 * width, lanes), jnp.float32),
            pltpu.VMEM((3, rows_out + 2 * width, lanes), jnp.float32),
        ],
    )(speeds, weights, spectrum, flow_fields, before, after, before, after, factor)


def halo_pieces(x, axis, dim, width):
    size, length = (lax.axis_size(axis), x.shape[dim])
    up = [(i, (i + 1) % size) for i in range(size - 1)]
    down = [(j, i) for i, j in up]
    last = lax.slice_in_dim(x, length - width, length, axis=dim)
    leading = lax.slice_in_dim(x, 0, width, axis=dim)
    return lax.ppermute(last, axis, up), lax.ppermute(leading, axis, down)

def pick_matmul(values, pick):
    parts = []
    rest = values
    for _ in range(2):
        head = lax.reduce_precision(rest, exponent_bits=8, mantissa_bits=7)
        parts.append(head)
        rest = rest - head
    parts.append(rest)
    rows = values.shape[0]
    stacked = jnp.concatenate(parts, 0).astype(jnp.bfloat16)
    product = jnp.dot(stacked, pick, preferred_element_type=jnp.float32)
    return (product[:rows] + product[rows : 2 * rows]) + product[2 * rows :]


def local(
    spectrum, courant, group_ratio, ocean_currents, elevation, sea_mask, owner_tile, ocean_slot
):
    bin_count, row_count, columns = spectrum.shape
    cell_count = row_count * columns
    tile_count = lax.axis_size("tile")
    capacity = 2 * ((cell_count + tile_count - 1) // tile_count)
    ocean_cells = elevation.shape[0]
    first_bin = lax.axis_index("sect") * bin_count
    bin_ids = first_bin + jnp.arange(bin_count, dtype=jnp.int32)
    dir_ids = bin_ids // NFREQ
    freq_ids = bin_ids % NFREQ
    freq_pick = (freq_ids[:, None] == jnp.arange(NFREQ, dtype=jnp.int32)[None, :]).astype(
        jnp.float32
    )
    group_speed = jnp.sum(freq_pick * courant[None, :], 1)
    ratio_bin = jnp.sum(freq_pick * group_ratio[None, :], 1)
    angles = (dir_ids.astype(jnp.float32) + 0.5) * (2.0 * math.pi / NDIR)
    cos_dir = jnp.cos(angles)
    sin_dir = jnp.sin(angles)
    owners = owner_tile[:, 0]
    cell_ids = jnp.arange(owners.shape[0], dtype=jnp.int32)
    same_before = (owners[None, :] == owners[:, None]) & (cell_ids[None, :] < cell_ids[:, None])
    rank_in = jnp.sum(same_before.astype(jnp.int32), 1)
    position = owners * capacity + rank_in
    slot_ids = jnp.arange(tile_count * capacity, dtype=jnp.int32)
    requests = (
        jnp.sum(jnp.where(position[:, None] == slot_ids[None, :], ocean_slot[:, None] + 1, 0), 0) - 1
    )
    asked_slots = lax.all_to_all(
        requests.reshape(tile_count, capacity), "tile", split_axis=0, concat_axis=0, tiled=True
    )
    is_valid = asked_slots >= 0
    surface = jnp.concatenate([ocean_currents, elevation[None]], 0)
    ocean_ids = jnp.arange(ocean_cells, dtype=jnp.int32)
    slot_pick = (ocean_ids[:, None] == asked_slots.reshape(-1)[None, :]).astype(jnp.bfloat16)
    answer = pick_matmul(surface, slot_pick).reshape(3, tile_count, capacity)
    returned = lax.all_to_all(answer, "tile", split_axis=1, concat_axis=1, tiled=True)
    cell_pick = (slot_ids[:, None] == position[None, :]).astype(jnp.bfloat16)
    at_cells = pick_matmul(returned.reshape(3, tile_count * capacity), cell_pick)
    sea_float = sea_mask.astype(jnp.float32)
    flow_fields = jnp.concatenate([at_cells[:2].reshape(2, row_count, columns), sea_float[None]], 0)
    before, after = halo_pieces(jnp.concatenate([spectrum, flow_fields], 0), "tile", 1, STEPS)
    speeds = jnp.stack([group_speed * cos_dir, group_speed * sin_dir], 0)
    weights = jnp.stack(
        [
            ratio_bin * (1.0 + cos_dir * cos_dir) - 0.5,
            ratio_bin * cos_dir * sin_dir,
            ratio_bin * (1.0 + sin_dir * sin_dir) - 0.5,
        ],
        0,
    ) * (4.0 / (NDIR * NFREQ))
    factor = ((1.0 + at_cells[2]) * sea_float.reshape(-1)).reshape(row_count, columns)
    energy, partial_value = propagate(
        speeds, weights, spectrum, flow_fields, before, after, factor
    )
    partial_value = partial_value.reshape(3, cell_count)
    sect_count = lax.axis_size("sect")
    every_part = lax.all_to_all(
        jnp.broadcast_to(partial_value[None], (sect_count,) + partial_value.shape),
        "sect",
        0,
        0,
        tiled=True,
    )
    partial_value = every_part[0]
    for part in range(1, sect_count):
        partial_value = partial_value + every_part[part]
    packed = pick_matmul(partial_value, cell_pick.T)
    arrived = lax.all_to_all(
        packed.reshape(3, tile_count, capacity), "tile", split_axis=1, concat_axis=1, tiled=True
    )
    weight = is_valid.reshape(-1).astype(jnp.float32)
    summed = pick_matmul(
        jnp.concatenate([arrived.reshape(3, -1) * weight[None], weight[None]], 0), slot_pick.T
    )
    return (energy, summed[:3] / jnp.maximum(summed[3], 1.0)[None])


def solution(mesh):
    in_specs = (
        P("sect", "tile", None),
        P(),
        P(),
        P(None, "tile"),
        P("tile"),
        P("tile", None),
        P("tile", None),
        P("tile"),
    )
    out_specs = (P("sect", "tile", None), P(None, "tile"))
    return jax.shard_map(local, mesh=mesh, in_specs=in_specs, out_specs=out_specs, check_vma=False)
```

```python
import functools
import math

import jax
import jax.numpy as jnp
from jax import lax
from jax.experimental import pallas as pl
from jax.experimental.pallas import tpu as pltpu
from jax.sharding import PartitionSpec as P

NDIR = 36
NFREQ = 36
STEPS = 4


def with_halo(x, sides, width):
    for axis, dim in sides:
        size, length = (lax.axis_size(axis), x.shape[dim])
        up = [(i, (i + 1) % size) for i in range(size - 1)]
        down = [(j, i) for i, j in up]
        last = lax.slice_in_dim(x, length - width, length, axis=dim)
        leading = lax.slice_in_dim(x, 0, width, axis=dim)
        before = lax.ppermute(last, axis, up)
        after = lax.ppermute(leading, axis, down)
        x = jnp.concatenate([before, x, after], axis=dim)
    return x


def advance(energy, flow_fields, speed_x, speed_y):
    vel_x = speed_x + flow_fields[0]
    vel_y = speed_y + flow_fields[1]
    middle = energy[:, 1:-1]
    mid_vel = vel_x[:, 1:-1]
    face_x = 0.5 * (mid_vel + jnp.roll(mid_vel, -1, axis=2))
    east_side = jnp.roll(middle, -1, axis=2)
    flux_x = jnp.maximum(face_x, 0.0) * middle + jnp.minimum(face_x, 0.0) * east_side
    div_x = flux_x - jnp.roll(flux_x, 1, axis=2)
    face_y = 0.5 * (vel_y[:, :-1] + vel_y[:, 1:])
    flux_y = jnp.maximum(face_y, 0.0) * energy[:, :-1] + jnp.minimum(face_y, 0.0) * energy[:, 1:]
    div_y = flux_y[:, 1:] - flux_y[:, :-1]
    return flow_fields[2, 1:-1] * (middle - div_x - div_y)


def propagate_kernel(
    speed_ref,
    weight_ref,
    energy_ref,
    flow_ref,
    before_ref,
    after_ref,
    flow_before_ref,
    flow_after_ref,
    factor_ref,
    out_ref,
    stress_ref,
    window_ref,
    flow_window_ref,
    *,
    block,
    steps,
):
    rows_out = energy_ref.shape[1]
    width = before_ref.shape[1]
    rows = rows_out + 2 * width
    lanes = energy_ref.shape[2]
    base = pl.program_id(0) * block

    @pl.when(pl.program_id(0) == 0)
    def _():
        stress_ref[0] = jnp.zeros(stress_ref.shape[1:], jnp.float32)

    flow_window_ref[:, :rows_out] = flow_ref[...]
    flow_window_ref[:, rows_out : rows_out + width] = flow_after_ref[...]
    flow_window_ref[:, rows_out + width :] = flow_before_ref[...]
    u = flow_window_ref[0]
    v = flow_window_ref[1]
    m = flow_window_ref[2]

    def one_bin(b, carry):
        window_ref[b, :rows_out] = energy_ref[b]
        window_ref[b, rows_out : rows_out + width] = after_ref[b]
        window_ref[b, rows_out + width :] = before_ref[b]
        vel_x = speed_ref[0, base + b] + u
        vel_y = speed_ref[1, base + b] + v
        face_x = 0.5 * (vel_x + pltpu.roll(vel_x, lanes - 1, 1))
        face_y = 0.5 * (vel_y + pltpu.roll(vel_y, rows - 1, 0))
        pos_x = jnp.maximum(face_x, 0.0)
        neg_x = jnp.minimum(face_x, 0.0)
        pos_y = jnp.maximum(face_y, 0.0)
        neg_y = jnp.minimum(face_y, 0.0)
        energy = window_ref[b]
        for _ in range(steps):
            flux_x = pos_x * energy + neg_x * pltpu.roll(energy, lanes - 1, 1)
            div_x = flux_x - pltpu.roll(flux_x, 1, 1)
            flux_y = pos_y * energy + neg_y * pltpu.roll(energy, rows - 1, 0)
            div_y = flux_y - pltpu.roll(flux_y, 1, 0)
            energy = m * (energy - div_x - div_y)
        kept = energy[:rows_out]
        out_ref[b] = kept
        return tuple(carry[k] + weight_ref[k, base + b] * kept for k in range(3))

    zero = jnp.zeros((rows_out, lanes), jnp.float32)
    sums = lax.fori_loop(0, block, one_bin, (zero, zero, zero), unroll=True)
    for k in range(3):
        stress_ref[0, k] = stress_ref[0, k] + sums[k]

    @pl.when(pl.program_id(0) == pl.num_programs(0) - 1)
    def _():
        for k in range(3):
            scaled = stress_ref[0, k] * factor_ref[...]
            for copy in range(stress_ref.shape[0]):
                stress_ref[copy, k] = scaled


def propagate(speeds, weights, spectrum, flow_fields, before, after, factor, copies):
    bins, rows_out, lanes = spectrum.shape
    width = before.shape[1]
    block = max(d for d in range(1, 33) if bins % d == 0)
    kernel = functools.partial(propagate_kernel, block=block, steps=STEPS)
    flows_at = bins // 3
    return pl.pallas_call(
        kernel,
        grid=(bins // block,),
        in_specs=[
            pl.BlockSpec(memory_space=pltpu.MemorySpace.SMEM),
            pl.BlockSpec(memory_space=pltpu.MemorySpace.SMEM),
            pl.BlockSpec((block, rows_out, lanes), lambda i: (i, 0, 0)),
            pl.BlockSpec((3, rows_out, lanes), lambda i: (0, 0, 0)),
            pl.BlockSpec((block, width, lanes), lambda i: (i, 0, 0)),
            pl.BlockSpec((block, width, lanes), lambda i: (i, 0, 0)),
            pl.BlockSpec((3, width, lanes), lambda i: (flows_at, 0, 0)),
            pl.BlockSpec((3, width, lanes), lambda i: (flows_at, 0, 0)),
            pl.BlockSpec((rows_out, lanes), lambda i: (0, 0)),
        ],
        out_specs=[
            pl.BlockSpec((block, rows_out, lanes), lambda i: (i, 0, 0)),
            pl.BlockSpec((copies, 3, rows_out, lanes), lambda i: (0, 0, 0, 0)),
        ],
        out_shape=[
            jax.ShapeDtypeStruct((bins, rows_out, lanes), jnp.float32),
            jax.ShapeDtypeStruct((copies, 3, rows_out, lanes), jnp.float32),
        ],
        scratch_shapes=[
            pltpu.VMEM((block, rows_out + 2 * width, lanes), jnp.float32),
            pltpu.VMEM((3, rows_out + 2 * width, lanes), jnp.float32),
        ],
    )(speeds, weights, spectrum, flow_fields, before, after, before, after, factor)


def halo_pieces(x, axis, dim, width):
    size, length = (lax.axis_size(axis), x.shape[dim])
    up = [(i, (i + 1) % size) for i in range(size - 1)]
    down = [(j, i) for i, j in up]
    last = lax.slice_in_dim(x, length - width, length, axis=dim)
    leading = lax.slice_in_dim(x, 0, width, axis=dim)
    return lax.ppermute(last, axis, up), lax.ppermute(leading, axis, down)

def pick_matmul(values, pick):
    parts = []
    rest = values
    for _ in range(2):
        head = lax.reduce_precision(rest, exponent_bits=8, mantissa_bits=7)
        parts.append(head)
        rest = rest - head
    parts.append(rest)
    rows = values.shape[0]
    stacked = jnp.concatenate(parts, 0).astype(jnp.bfloat16)
    product = jnp.dot(stacked, pick, preferred_element_type=jnp.float32)
    return (product[:rows] + product[rows : 2 * rows]) + product[2 * rows :]


def local(
    spectrum, courant, group_ratio, ocean_currents, elevation, sea_mask, owner_tile, ocean_slot
):
    bin_count, row_count, columns = spectrum.shape
    cell_count = row_count * columns
    tile_count = lax.axis_size("tile")
    capacity = 2 * ((cell_count + tile_count - 1) // tile_count)
    ocean_cells = elevation.shape[0]
    first_bin = lax.axis_index("sect") * bin_count
    bin_ids = first_bin + jnp.arange(bin_count, dtype=jnp.int32)
    dir_ids = bin_ids // NFREQ
    freq_ids = bin_ids % NFREQ
    freq_pick = (freq_ids[:, None] == jnp.arange(NFREQ, dtype=jnp.int32)[None, :]).astype(
        jnp.float32
    )
    group_speed = jnp.sum(freq_pick * courant[None, :], 1)
    ratio_bin = jnp.sum(freq_pick * group_ratio[None, :], 1)
    angles = (dir_ids.astype(jnp.float32) + 0.5) * (2.0 * math.pi / NDIR)
    cos_dir = jnp.cos(angles)
    sin_dir = jnp.sin(angles)
    owners = owner_tile[:, 0]
    cell_ids = jnp.arange(owners.shape[0], dtype=jnp.int32)
    same_before = (owners[None, :] == owners[:, None]) & (cell_ids[None, :] < cell_ids[:, None])
    rank_in = jnp.sum(same_before.astype(jnp.int32), 1)
    position = owners * capacity + rank_in
    slot_ids = jnp.arange(tile_count * capacity, dtype=jnp.int32)
    requests = (
        jnp.sum(jnp.where(position[:, None] == slot_ids[None, :], ocean_slot[:, None] + 1, 0), 0) - 1
    )
    asked_slots = lax.all_to_all(
        requests.reshape(tile_count, capacity), "tile", split_axis=0, concat_axis=0, tiled=True
    )
    is_valid = asked_slots >= 0
    surface = jnp.concatenate([ocean_currents, elevation[None]], 0)
    ocean_ids = jnp.arange(ocean_cells, dtype=jnp.int32)
    slot_pick = (ocean_ids[:, None] == asked_slots.reshape(-1)[None, :]).astype(jnp.bfloat16)
    answer = pick_matmul(surface, slot_pick).reshape(3, tile_count, capacity)
    returned = lax.all_to_all(answer, "tile", split_axis=1, concat_axis=1, tiled=True)
    cell_pick = (slot_ids[:, None] == position[None, :]).astype(jnp.bfloat16)
    at_cells = pick_matmul(returned.reshape(3, tile_count * capacity), cell_pick)
    sea_float = sea_mask.astype(jnp.float32)
    flow_fields = jnp.concatenate([at_cells[:2].reshape(2, row_count, columns), sea_float[None]], 0)
    before, after = halo_pieces(jnp.concatenate([spectrum, flow_fields], 0), "tile", 1, STEPS)
    speeds = jnp.stack([group_speed * cos_dir, group_speed * sin_dir], 0)
    weights = jnp.stack(
        [
            ratio_bin * (1.0 + cos_dir * cos_dir) - 0.5,
            ratio_bin * cos_dir * sin_dir,
            ratio_bin * (1.0 + sin_dir * sin_dir) - 0.5,
        ],
        0,
    ) * (4.0 / (NDIR * NFREQ))
    factor = ((1.0 + at_cells[2]) * sea_float.reshape(-1)).reshape(row_count, columns)
    sect_count = lax.axis_size("sect")
    energy, partial_copies = propagate(
        speeds, weights, spectrum, flow_fields, before, after, factor, sect_count
    )
    every_part = lax.all_to_all(partial_copies, "sect", 0, 0, tiled=True)
    partial_value = every_part[0]
    for part in range(1, sect_count):
        partial_value = partial_value + every_part[part]
    partial_value = partial_value.reshape(3, cell_count)
    packed = pick_matmul(partial_value, cell_pick.T)
    arrived = lax.all_to_all(
        packed.reshape(3, tile_count, capacity), "tile", split_axis=1, concat_axis=1, tiled=True
    )
    weight = is_valid.reshape(-1).astype(jnp.float32)
    summed = pick_matmul(
        jnp.concatenate([arrived.reshape(3, -1) * weight[None], weight[None]], 0), slot_pick.T
    )
    return (energy, summed[:3] / jnp.maximum(summed[3], 1.0)[None])


def solution(mesh):
    in_specs = (
        P("sect", "tile", None),
        P(),
        P(),
        P(None, "tile"),
        P("tile"),
        P("tile", None),
        P("tile", None),
        P("tile"),
    )
    out_specs = (P("sect", "tile", None), P(None, "tile"))
    return jax.shard_map(local, mesh=mesh, in_specs=in_specs, out_specs=out_specs, check_vma=False)
```

```python
import functools
import math

import jax
import jax.numpy as jnp
from jax import lax
from jax.experimental import pallas as pl
from jax.experimental.pallas import tpu as pltpu
from jax.sharding import PartitionSpec as P

NDIR = 36
NFREQ = 36
STEPS = 4


def with_halo(x, sides, width):
    for axis, dim in sides:
        size, length = (lax.axis_size(axis), x.shape[dim])
        up = [(i, (i + 1) % size) for i in range(size - 1)]
        down = [(j, i) for i, j in up]
        last = lax.slice_in_dim(x, length - width, length, axis=dim)
        leading = lax.slice_in_dim(x, 0, width, axis=dim)
        before = lax.ppermute(last, axis, up)
        after = lax.ppermute(leading, axis, down)
        x = jnp.concatenate([before, x, after], axis=dim)
    return x


def advance(energy, flow_fields, speed_x, speed_y):
    vel_x = speed_x + flow_fields[0]
    vel_y = speed_y + flow_fields[1]
    middle = energy[:, 1:-1]
    mid_vel = vel_x[:, 1:-1]
    face_x = 0.5 * (mid_vel + jnp.roll(mid_vel, -1, axis=2))
    east_side = jnp.roll(middle, -1, axis=2)
    flux_x = jnp.maximum(face_x, 0.0) * middle + jnp.minimum(face_x, 0.0) * east_side
    div_x = flux_x - jnp.roll(flux_x, 1, axis=2)
    face_y = 0.5 * (vel_y[:, :-1] + vel_y[:, 1:])
    flux_y = jnp.maximum(face_y, 0.0) * energy[:, :-1] + jnp.minimum(face_y, 0.0) * energy[:, 1:]
    div_y = flux_y[:, 1:] - flux_y[:, :-1]
    return flow_fields[2, 1:-1] * (middle - div_x - div_y)


def propagate_kernel(
    speed_ref,
    weight_ref,
    energy_ref,
    flow_ref,
    before_ref,
    after_ref,
    flow_before_ref,
    flow_after_ref,
    factor_ref,
    out_ref,
    stress_ref,
    window_ref,
    flow_window_ref,
    *,
    block,
    steps,
):
    rows_out = energy_ref.shape[1]
    width = before_ref.shape[1]
    rows = rows_out + 2 * width
    lanes = energy_ref.shape[2]
    base = pl.program_id(0) * block

    @pl.when(pl.program_id(0) == 0)
    def _():
        stress_ref[0] = jnp.zeros(stress_ref.shape[1:], jnp.float32)

    flow_window_ref[:, :rows_out] = flow_ref[...]
    flow_window_ref[:, rows_out : rows_out + width] = flow_after_ref[...]
    flow_window_ref[:, rows_out + width :] = flow_before_ref[...]
    u = flow_window_ref[0]
    v = flow_window_ref[1]
    m = flow_window_ref[2]

    def one_bin(b, carry):
        window_ref[b, :rows_out] = energy_ref[b]
        window_ref[b, rows_out : rows_out + width] = after_ref[b]
        window_ref[b, rows_out + width :] = before_ref[b]
        vel_x = speed_ref[0, base + b] + u
        vel_y = speed_ref[1, base + b] + v
        face_x = 0.5 * (vel_x + pltpu.roll(vel_x, lanes - 1, 1))
        face_y = 0.5 * (vel_y + pltpu.roll(vel_y, rows - 1, 0))
        pos_x = jnp.maximum(face_x, 0.0)
        neg_x = jnp.minimum(face_x, 0.0)
        pos_y = jnp.maximum(face_y, 0.0)
        neg_y = jnp.minimum(face_y, 0.0)
        energy = window_ref[b]
        for _ in range(steps):
            flux_x = pos_x * energy + neg_x * pltpu.roll(energy, lanes - 1, 1)
            div_x = flux_x - pltpu.roll(flux_x, 1, 1)
            flux_y = pos_y * energy + neg_y * pltpu.roll(energy, rows - 1, 0)
            div_y = flux_y - pltpu.roll(flux_y, 1, 0)
            energy = m * (energy - div_x - div_y)
        kept = energy[:rows_out]
        out_ref[b] = kept
        return tuple(carry[k] + weight_ref[k, base + b] * kept for k in range(3))

    zero = jnp.zeros((rows_out, lanes), jnp.float32)
    sums = lax.fori_loop(0, block, one_bin, (zero, zero, zero), unroll=True)
    for k in range(3):
        stress_ref[0, k] = stress_ref[0, k] + sums[k]

    @pl.when(pl.program_id(0) == pl.num_programs(0) - 1)
    def _():
        for k in range(3):
            scaled = stress_ref[0, k] * factor_ref[...]
            for copy in range(stress_ref.shape[0]):
                stress_ref[copy, k] = scaled


def propagate(speeds, weights, spectrum, flow_fields, before, after, factor, copies):
    bins, rows_out, lanes = spectrum.shape
    width = before.shape[1]
    block = max(d for d in range(1, 33) if bins % d == 0)
    kernel = functools.partial(propagate_kernel, block=block, steps=STEPS)
    flows_at = bins // 3
    return pl.pallas_call(
        kernel,
        grid=(bins // block,),
        in_specs=[
            pl.BlockSpec(memory_space=pltpu.MemorySpace.SMEM),
            pl.BlockSpec(memory_space=pltpu.MemorySpace.SMEM),
            pl.BlockSpec((block, rows_out, lanes), lambda i: (i, 0, 0)),
            pl.BlockSpec((3, rows_out, lanes), lambda i: (0, 0, 0)),
            pl.BlockSpec((block, width, lanes), lambda i: (i, 0, 0)),
            pl.BlockSpec((block, width, lanes), lambda i: (i, 0, 0)),
            pl.BlockSpec((3, width, lanes), lambda i: (flows_at, 0, 0)),
            pl.BlockSpec((3, width, lanes), lambda i: (flows_at, 0, 0)),
            pl.BlockSpec((rows_out, lanes), lambda i: (0, 0)),
        ],
        out_specs=[
            pl.BlockSpec((block, rows_out, lanes), lambda i: (i, 0, 0)),
            pl.BlockSpec((copies, 3, rows_out, lanes), lambda i: (0, 0, 0, 0)),
        ],
        out_shape=[
            jax.ShapeDtypeStruct((bins, rows_out, lanes), jnp.float32),
            jax.ShapeDtypeStruct((copies, 3, rows_out, lanes), jnp.float32),
        ],
        scratch_shapes=[
            pltpu.VMEM((block, rows_out + 2 * width, lanes), jnp.float32),
            pltpu.VMEM((3, rows_out + 2 * width, lanes), jnp.float32),
        ],
    )(speeds, weights, spectrum, flow_fields, before, after, before, after, factor)


def halo_pieces(x, axis, dim, width):
    size, length = (lax.axis_size(axis), x.shape[dim])
    up = [(i, (i + 1) % size) for i in range(size - 1)]
    down = [(j, i) for i, j in up]
    last = lax.slice_in_dim(x, length - width, length, axis=dim)
    leading = lax.slice_in_dim(x, 0, width, axis=dim)
    return lax.ppermute(last, axis, up), lax.ppermute(leading, axis, down)

def pick_matmul(values, pick):
    parts = []
    rest = values
    for _ in range(2):
        head = lax.reduce_precision(rest, exponent_bits=8, mantissa_bits=7)
        parts.append(head)
        rest = rest - head
    parts.append(rest)
    rows = values.shape[0]
    stacked = jnp.concatenate(parts, 0).astype(jnp.bfloat16)
    product = jnp.dot(stacked, pick, preferred_element_type=jnp.float32)
    return (product[:rows] + product[rows : 2 * rows]) + product[2 * rows :]


def local(
    spectrum, courant, group_ratio, ocean_currents, elevation, sea_mask, owner_tile, ocean_slot
):
    bin_count, row_count, columns = spectrum.shape
    cell_count = row_count * columns
    tile_count = lax.axis_size("tile")
    capacity = 2 * ((cell_count + tile_count - 1) // tile_count)
    ocean_cells = elevation.shape[0]
    first_bin = lax.axis_index("sect") * bin_count
    bin_ids = first_bin + jnp.arange(bin_count, dtype=jnp.int32)
    dir_ids = bin_ids // NFREQ
    freq_ids = bin_ids % NFREQ
    freq_pick = (freq_ids[:, None] == jnp.arange(NFREQ, dtype=jnp.int32)[None, :]).astype(
        jnp.float32
    )
    group_speed = jnp.sum(freq_pick * courant[None, :], 1)
    ratio_bin = jnp.sum(freq_pick * group_ratio[None, :], 1)
    angles = (dir_ids.astype(jnp.float32) + 0.5) * (2.0 * math.pi / NDIR)
    cos_dir = jnp.cos(angles)
    sin_dir = jnp.sin(angles)
    owners = owner_tile[:, 0]
    cell_ids = jnp.arange(owners.shape[0], dtype=jnp.int32)
    earlier = (cell_ids[None, :] < cell_ids[:, None]).astype(jnp.bfloat16)
    owner_pick = owners[:, None] == jnp.arange(tile_count, dtype=jnp.int32)[None, :]
    seen = jnp.dot(earlier, owner_pick.astype(jnp.bfloat16), preferred_element_type=jnp.float32)
    rank_in = jnp.sum(jnp.where(owner_pick, seen, 0.0), 1).astype(jnp.int32)
    position = owners * capacity + rank_in
    slot_ids = jnp.arange(tile_count * capacity, dtype=jnp.int32)
    requests = (
        jnp.sum(jnp.where(position[:, None] == slot_ids[None, :], ocean_slot[:, None] + 1, 0), 0) - 1
    )
    asked_slots = lax.all_to_all(
        requests.reshape(tile_count, capacity), "tile", split_axis=0, concat_axis=0, tiled=True
    )
    is_valid = asked_slots >= 0
    surface = jnp.concatenate([ocean_currents, elevation[None]], 0)
    ocean_ids = jnp.arange(ocean_cells, dtype=jnp.int32)
    slot_pick = (ocean_ids[:, None] == asked_slots.reshape(-1)[None, :]).astype(jnp.bfloat16)
    answer = pick_matmul(surface, slot_pick).reshape(3, tile_count, capacity)
    returned = lax.all_to_all(answer, "tile", split_axis=1, concat_axis=1, tiled=True)
    cell_pick = (slot_ids[:, None] == position[None, :]).astype(jnp.bfloat16)
    at_cells = pick_matmul(returned.reshape(3, tile_count * capacity), cell_pick)
    sea_float = sea_mask.astype(jnp.float32)
    flow_fields = jnp.concatenate([at_cells[:2].reshape(2, row_count, columns), sea_float[None]], 0)
    before, after = halo_pieces(jnp.concatenate([spectrum, flow_fields], 0), "tile", 1, STEPS)
    speeds = jnp.stack([group_speed * cos_dir, group_speed * sin_dir], 0)
    weights = jnp.stack(
        [
            ratio_bin * (1.0 + cos_dir * cos_dir) - 0.5,
            ratio_bin * cos_dir * sin_dir,
            ratio_bin * (1.0 + sin_dir * sin_dir) - 0.5,
        ],
        0,
    ) * (4.0 / (NDIR * NFREQ))
    factor = ((1.0 + at_cells[2]) * sea_float.reshape(-1)).reshape(row_count, columns)
    sect_count = lax.axis_size("sect")
    energy, partial_copies = propagate(
        speeds, weights, spectrum, flow_fields, before, after, factor, sect_count
    )
    every_part = lax.all_to_all(partial_copies, "sect", 0, 0, tiled=True)
    partial_value = every_part[0]
    for part in range(1, sect_count):
        partial_value = partial_value + every_part[part]
    partial_value = partial_value.reshape(3, cell_count)
    packed = pick_matmul(partial_value, cell_pick.T)
    arrived = lax.all_to_all(
        packed.reshape(3, tile_count, capacity), "tile", split_axis=1, concat_axis=1, tiled=True
    )
    weight = is_valid.reshape(-1).astype(jnp.float32)
    summed = pick_matmul(
        jnp.concatenate([arrived.reshape(3, -1) * weight[None], weight[None]], 0), slot_pick.T
    )
    return (energy, summed[:3] / jnp.maximum(summed[3], 1.0)[None])


def solution(mesh):
    in_specs = (
        P("sect", "tile", None),
        P(),
        P(),
        P(None, "tile"),
        P("tile"),
        P("tile", None),
        P("tile", None),
        P("tile"),
    )
    out_specs = (P("sect", "tile", None), P(None, "tile"))
    return jax.shard_map(local, mesh=mesh, in_specs=in_specs, out_specs=out_specs, check_vma=False)
```

```python
import functools
import math

import jax
import jax.numpy as jnp
from jax import lax
from jax.experimental import pallas as pl
from jax.experimental.pallas import tpu as pltpu
from jax.sharding import PartitionSpec as P

NDIR = 36
NFREQ = 36
STEPS = 4


def with_halo(x, sides, width):
    for axis, dim in sides:
        size, length = (lax.axis_size(axis), x.shape[dim])
        up = [(i, (i + 1) % size) for i in range(size - 1)]
        down = [(j, i) for i, j in up]
        last = lax.slice_in_dim(x, length - width, length, axis=dim)
        leading = lax.slice_in_dim(x, 0, width, axis=dim)
        before = lax.ppermute(last, axis, up)
        after = lax.ppermute(leading, axis, down)
        x = jnp.concatenate([before, x, after], axis=dim)
    return x


def advance(energy, flow_fields, speed_x, speed_y):
    vel_x = speed_x + flow_fields[0]
    vel_y = speed_y + flow_fields[1]
    middle = energy[:, 1:-1]
    mid_vel = vel_x[:, 1:-1]
    face_x = 0.5 * (mid_vel + jnp.roll(mid_vel, -1, axis=2))
    east_side = jnp.roll(middle, -1, axis=2)
    flux_x = jnp.maximum(face_x, 0.0) * middle + jnp.minimum(face_x, 0.0) * east_side
    div_x = flux_x - jnp.roll(flux_x, 1, axis=2)
    face_y = 0.5 * (vel_y[:, :-1] + vel_y[:, 1:])
    flux_y = jnp.maximum(face_y, 0.0) * energy[:, :-1] + jnp.minimum(face_y, 0.0) * energy[:, 1:]
    div_y = flux_y[:, 1:] - flux_y[:, :-1]
    return flow_fields[2, 1:-1] * (middle - div_x - div_y)


def propagate_kernel(
    speed_ref,
    weight_ref,
    energy_ref,
    flow_ref,
    before_ref,
    after_ref,
    flow_before_ref,
    flow_after_ref,
    factor_ref,
    out_ref,
    stress_ref,
    window_ref,
    flow_window_ref,
    *,
    block,
    steps,
):
    rows_out = energy_ref.shape[1]
    width = before_ref.shape[1]
    rows = rows_out + 2 * width
    lanes = energy_ref.shape[2]
    base = pl.program_id(0) * block

    @pl.when(pl.program_id(0) == 0)
    def _():
        stress_ref[0] = jnp.zeros(stress_ref.shape[1:], jnp.float32)

    flow_window_ref[:, :rows_out] = flow_ref[...]
    flow_window_ref[:, rows_out : rows_out + width] = flow_after_ref[...]
    flow_window_ref[:, rows_out + width :] = flow_before_ref[...]
    u = flow_window_ref[0]
    v = flow_window_ref[1]
    m = flow_window_ref[2]

    def one_bin(b, carry):
        window_ref[b, :rows_out] = energy_ref[b]
        window_ref[b, rows_out : rows_out + width] = after_ref[b]
        window_ref[b, rows_out + width :] = before_ref[b]
        vel_x = speed_ref[0, base + b] + u
        vel_y = speed_ref[1, base + b] + v
        face_x = 0.5 * (vel_x + pltpu.roll(vel_x, lanes - 1, 1))
        face_y = 0.5 * (vel_y + pltpu.roll(vel_y, rows - 1, 0))
        pos_x = jnp.maximum(face_x, 0.0)
        neg_x = jnp.minimum(face_x, 0.0)
        pos_y = jnp.maximum(face_y, 0.0)
        neg_y = jnp.minimum(face_y, 0.0)
        energy = window_ref[b]
        for _ in range(steps):
            flux_x = pos_x * energy + neg_x * pltpu.roll(energy, lanes - 1, 1)
            div_x = flux_x - pltpu.roll(flux_x, 1, 1)
            flux_y = pos_y * energy + neg_y * pltpu.roll(energy, rows - 1, 0)
            div_y = flux_y - pltpu.roll(flux_y, 1, 0)
            energy = m * (energy - div_x - div_y)
        kept = energy[:rows_out]
        out_ref[b] = kept
        return tuple(carry[k] + weight_ref[k, base + b] * kept for k in range(3))

    zero = jnp.zeros((rows_out, lanes), jnp.float32)
    sums = lax.fori_loop(0, block, one_bin, (zero, zero, zero), unroll=True)
    for k in range(3):
        stress_ref[0, k] = stress_ref[0, k] + sums[k]

    @pl.when(pl.program_id(0) == pl.num_programs(0) - 1)
    def _():
        for k in range(3):
            scaled = stress_ref[0, k] * factor_ref[...]
            for copy in range(stress_ref.shape[0]):
                stress_ref[copy, k] = scaled


def propagate(speeds, weights, spectrum, flow_fields, before, after, factor, copies):
    bins, rows_out, lanes = spectrum.shape
    width = before.shape[1]
    block = max(d for d in range(1, 33) if bins % d == 0)
    kernel = functools.partial(propagate_kernel, block=block, steps=STEPS)
    flows_at = bins // 3
    return pl.pallas_call(
        kernel,
        grid=(bins // block,),
        in_specs=[
            pl.BlockSpec(memory_space=pltpu.MemorySpace.SMEM),
            pl.BlockSpec(memory_space=pltpu.MemorySpace.SMEM),
            pl.BlockSpec((block, rows_out, lanes), lambda i: (i, 0, 0)),
            pl.BlockSpec((3, rows_out, lanes), lambda i: (0, 0, 0)),
            pl.BlockSpec((block, width, lanes), lambda i: (i, 0, 0)),
            pl.BlockSpec((block, width, lanes), lambda i: (i, 0, 0)),
            pl.BlockSpec((3, width, lanes), lambda i: (flows_at, 0, 0)),
            pl.BlockSpec((3, width, lanes), lambda i: (flows_at, 0, 0)),
            pl.BlockSpec((rows_out, lanes), lambda i: (0, 0)),
        ],
        out_specs=[
            pl.BlockSpec((block, rows_out, lanes), lambda i: (i, 0, 0)),
            pl.BlockSpec((copies, 3, rows_out, lanes), lambda i: (0, 0, 0, 0)),
        ],
        out_shape=[
            jax.ShapeDtypeStruct((bins, rows_out, lanes), jnp.float32),
            jax.ShapeDtypeStruct((copies, 3, rows_out, lanes), jnp.float32),
        ],
        scratch_shapes=[
            pltpu.VMEM((block, rows_out + 2 * width, lanes), jnp.float32),
            pltpu.VMEM((3, rows_out + 2 * width, lanes), jnp.float32),
        ],
    )(speeds, weights, spectrum, flow_fields, before, after, before, after, factor)


def halo_pieces(x, axis, dim, width):
    size, length = (lax.axis_size(axis), x.shape[dim])
    up = [(i, (i + 1) % size) for i in range(size - 1)]
    down = [(j, i) for i, j in up]
    last = lax.slice_in_dim(x, length - width, length, axis=dim)
    leading = lax.slice_in_dim(x, 0, width, axis=dim)
    return lax.ppermute(last, axis, up), lax.ppermute(leading, axis, down)

def pick_matmul(values, pick):
    parts = []
    rest = values
    for _ in range(2):
        head = lax.reduce_precision(rest, exponent_bits=8, mantissa_bits=7)
        parts.append(head)
        rest = rest - head
    parts.append(rest)
    rows = values.shape[0]
    stacked = jnp.concatenate(parts, 0).astype(jnp.bfloat16)
    product = jnp.dot(stacked, pick, preferred_element_type=jnp.float32)
    return (product[:rows] + product[rows : 2 * rows]) + product[2 * rows :]


def local(
    spectrum, courant, group_ratio, ocean_currents, elevation, sea_mask, owner_tile, ocean_slot
):
    bin_count, row_count, columns = spectrum.shape
    cell_count = row_count * columns
    tile_count = lax.axis_size("tile")
    capacity = 2 * ((cell_count + tile_count - 1) // tile_count)
    ocean_cells = elevation.shape[0]
    first_bin = lax.axis_index("sect") * bin_count
    bin_ids = first_bin + jnp.arange(bin_count, dtype=jnp.int32)
    dir_ids = bin_ids // NFREQ
    freq_ids = bin_ids % NFREQ
    freq_pick = (freq_ids[:, None] == jnp.arange(NFREQ, dtype=jnp.int32)[None, :]).astype(
        jnp.float32
    )
    group_speed = jnp.sum(freq_pick * courant[None, :], 1)
    ratio_bin = jnp.sum(freq_pick * group_ratio[None, :], 1)
    angles = (dir_ids.astype(jnp.float32) + 0.5) * (2.0 * math.pi / NDIR)
    cos_dir = jnp.cos(angles)
    sin_dir = jnp.sin(angles)
    owners = owner_tile[:, 0]
    cell_ids = jnp.arange(owners.shape[0], dtype=jnp.int32)
    earlier = (cell_ids[None, :] < cell_ids[:, None]).astype(jnp.bfloat16)
    owner_pick = owners[:, None] == jnp.arange(tile_count, dtype=jnp.int32)[None, :]
    seen = jnp.dot(earlier, owner_pick.astype(jnp.bfloat16), preferred_element_type=jnp.float32)
    rank_in = jnp.sum(jnp.where(owner_pick, seen, 0.0), 1).astype(jnp.int32)
    position = owners * capacity + rank_in
    slot_ids = jnp.arange(tile_count * capacity, dtype=jnp.int32)
    requests = jnp.max(
        jnp.where(position[:, None] == slot_ids[None, :], ocean_slot[:, None], -1), 0
    )
    asked_slots = lax.all_to_all(
        requests.reshape(tile_count, capacity), "tile", split_axis=0, concat_axis=0, tiled=True
    )
    is_valid = asked_slots >= 0
    surface = jnp.concatenate([ocean_currents, elevation[None]], 0)
    ocean_ids = jnp.arange(ocean_cells, dtype=jnp.int32)
    slot_pick = (ocean_ids[:, None] == asked_slots.reshape(-1)[None, :]).astype(jnp.bfloat16)
    answer = pick_matmul(surface, slot_pick).reshape(3, tile_count, capacity)
    returned = lax.all_to_all(answer, "tile", split_axis=1, concat_axis=1, tiled=True)
    cell_pick = (slot_ids[:, None] == position[None, :]).astype(jnp.bfloat16)
    at_cells = pick_matmul(returned.reshape(3, tile_count * capacity), cell_pick)
    sea_float = sea_mask.astype(jnp.float32)
    flow_fields = jnp.concatenate([at_cells[:2].reshape(2, row_count, columns), sea_float[None]], 0)
    before, after = halo_pieces(jnp.concatenate([spectrum, flow_fields], 0), "tile", 1, STEPS)
    speeds = jnp.stack([group_speed * cos_dir, group_speed * sin_dir], 0)
    weights = jnp.stack(
        [
            ratio_bin * (1.0 + cos_dir * cos_dir) - 0.5,
            ratio_bin * cos_dir * sin_dir,
            ratio_bin * (1.0 + sin_dir * sin_dir) - 0.5,
        ],
        0,
    ) * (4.0 / (NDIR * NFREQ))
    factor = ((1.0 + at_cells[2]) * sea_float.reshape(-1)).reshape(row_count, columns)
    sect_count = lax.axis_size("sect")
    energy, partial_copies = propagate(
        speeds, weights, spectrum, flow_fields, before, after, factor, sect_count
    )
    every_part = lax.all_to_all(partial_copies, "sect", 0, 0, tiled=True)
    partial_value = every_part[0]
    for part in range(1, sect_count):
        partial_value = partial_value + every_part[part]
    partial_value = partial_value.reshape(3, cell_count)
    packed = pick_matmul(partial_value, cell_pick.T)
    arrived = lax.all_to_all(
        packed.reshape(3, tile_count, capacity), "tile", split_axis=1, concat_axis=1, tiled=True
    )
    weight = is_valid.reshape(-1).astype(jnp.float32)
    summed = pick_matmul(
        jnp.concatenate([arrived.reshape(3, -1) * weight[None], weight[None]], 0), slot_pick.T
    )
    return (energy, summed[:3] / jnp.maximum(summed[3], 1.0)[None])


def solution(mesh):
    in_specs = (
        P("sect", "tile", None),
        P(),
        P(),
        P(None, "tile"),
        P("tile"),
        P("tile", None),
        P("tile", None),
        P("tile"),
    )
    out_specs = (P("sect", "tile", None), P(None, "tile"))
    return jax.shard_map(local, mesh=mesh, in_specs=in_specs, out_specs=out_specs, check_vma=False)
```

```python
import functools
import math

import jax
import jax.numpy as jnp
from jax import lax
from jax.experimental import pallas as pl
from jax.experimental.pallas import tpu as pltpu
from jax.sharding import PartitionSpec as P

NDIR = 36
NFREQ = 36
STEPS = 4


def with_halo(x, sides, width):
    for axis, dim in sides:
        size, length = (lax.axis_size(axis), x.shape[dim])
        up = [(i, (i + 1) % size) for i in range(size - 1)]
        down = [(j, i) for i, j in up]
        last = lax.slice_in_dim(x, length - width, length, axis=dim)
        leading = lax.slice_in_dim(x, 0, width, axis=dim)
        before = lax.ppermute(last, axis, up)
        after = lax.ppermute(leading, axis, down)
        x = jnp.concatenate([before, x, after], axis=dim)
    return x


def advance(energy, flow_fields, speed_x, speed_y):
    vel_x = speed_x + flow_fields[0]
    vel_y = speed_y + flow_fields[1]
    middle = energy[:, 1:-1]
    mid_vel = vel_x[:, 1:-1]
    face_x = 0.5 * (mid_vel + jnp.roll(mid_vel, -1, axis=2))
    east_side = jnp.roll(middle, -1, axis=2)
    flux_x = jnp.maximum(face_x, 0.0) * middle + jnp.minimum(face_x, 0.0) * east_side
    div_x = flux_x - jnp.roll(flux_x, 1, axis=2)
    face_y = 0.5 * (vel_y[:, :-1] + vel_y[:, 1:])
    flux_y = jnp.maximum(face_y, 0.0) * energy[:, :-1] + jnp.minimum(face_y, 0.0) * energy[:, 1:]
    div_y = flux_y[:, 1:] - flux_y[:, :-1]
    return flow_fields[2, 1:-1] * (middle - div_x - div_y)


def propagate_kernel(
    speed_ref,
    weight_ref,
    energy_ref,
    flow_ref,
    before_ref,
    after_ref,
    flow_before_ref,
    flow_after_ref,
    factor_ref,
    out_ref,
    stress_ref,
    window_ref,
    flow_window_ref,
    *,
    block,
    steps,
):
    rows_out = energy_ref.shape[1]
    width = before_ref.shape[1]
    rows = rows_out + 2 * width
    lanes = energy_ref.shape[2]
    base = pl.program_id(0) * block

    @pl.when(pl.program_id(0) == 0)
    def _():
        stress_ref[0] = jnp.zeros(stress_ref.shape[1:], jnp.float32)

    flow_window_ref[:, :rows_out] = flow_ref[...]
    flow_window_ref[:, rows_out : rows_out + width] = flow_after_ref[...]
    flow_window_ref[:, rows_out + width :] = flow_before_ref[...]
    u = flow_window_ref[0]
    v = flow_window_ref[1]
    m = flow_window_ref[2]

    def one_bin(b, carry):
        window_ref[b, :rows_out] = energy_ref[b]
        window_ref[b, rows_out : rows_out + width] = after_ref[b]
        window_ref[b, rows_out + width :] = before_ref[b]
        vel_x = speed_ref[0, base + b] + u
        vel_y = speed_ref[1, base + b] + v
        face_x = 0.5 * (vel_x + pltpu.roll(vel_x, lanes - 1, 1))
        face_y = 0.5 * (vel_y + pltpu.roll(vel_y, rows - 1, 0))
        pos_x = jnp.maximum(face_x, 0.0)
        neg_x = jnp.minimum(face_x, 0.0)
        pos_y = jnp.maximum(face_y, 0.0)
        neg_y = jnp.minimum(face_y, 0.0)
        energy = window_ref[b]
        for _ in range(steps):
            flux_x = pos_x * energy + neg_x * pltpu.roll(energy, lanes - 1, 1)
            div_x = flux_x - pltpu.roll(flux_x, 1, 1)
            flux_y = pos_y * energy + neg_y * pltpu.roll(energy, rows - 1, 0)
            div_y = flux_y - pltpu.roll(flux_y, 1, 0)
            energy = m * (energy - div_x - div_y)
        kept = energy[:rows_out]
        out_ref[b] = kept
        return tuple(carry[k] + weight_ref[k, base + b] * kept for k in range(3))

    zero = jnp.zeros((rows_out, lanes), jnp.float32)
    sums = lax.fori_loop(0, block, one_bin, (zero, zero, zero), unroll=True)
    for k in range(3):
        stress_ref[0, k] = stress_ref[0, k] + sums[k]

    @pl.when(pl.program_id(0) == pl.num_programs(0) - 1)
    def _():
        for k in range(3):
            scaled = stress_ref[0, k] * factor_ref[...]
            for copy in range(stress_ref.shape[0]):
                stress_ref[copy, k] = scaled


def propagate(speeds, weights, spectrum, flow_fields, before, after, factor, copies):
    bins, rows_out, lanes = spectrum.shape
    width = before.shape[1]
    block = max(d for d in range(1, 33) if bins % d == 0)
    kernel = functools.partial(propagate_kernel, block=block, steps=STEPS)
    flows_at = bins // 3
    return pl.pallas_call(
        kernel,
        grid=(bins // block,),
        in_specs=[
            pl.BlockSpec(memory_space=pltpu.MemorySpace.SMEM),
            pl.BlockSpec(memory_space=pltpu.MemorySpace.SMEM),
            pl.BlockSpec((block, rows_out, lanes), lambda i: (i, 0, 0)),
            pl.BlockSpec((3, rows_out, lanes), lambda i: (0, 0, 0)),
            pl.BlockSpec((block, width, lanes), lambda i: (i, 0, 0)),
            pl.BlockSpec((block, width, lanes), lambda i: (i, 0, 0)),
            pl.BlockSpec((3, width, lanes), lambda i: (flows_at, 0, 0)),
            pl.BlockSpec((3, width, lanes), lambda i: (flows_at, 0, 0)),
            pl.BlockSpec((rows_out, lanes), lambda i: (0, 0)),
        ],
        out_specs=[
            pl.BlockSpec((block, rows_out, lanes), lambda i: (i, 0, 0)),
            pl.BlockSpec((copies, 3, rows_out, lanes), lambda i: (0, 0, 0, 0)),
        ],
        out_shape=[
            jax.ShapeDtypeStruct((bins, rows_out, lanes), jnp.float32),
            jax.ShapeDtypeStruct((copies, 3, rows_out, lanes), jnp.float32),
        ],
        scratch_shapes=[
            pltpu.VMEM((block, rows_out + 2 * width, lanes), jnp.float32),
            pltpu.VMEM((3, rows_out + 2 * width, lanes), jnp.float32),
        ],
    )(speeds, weights, spectrum, flow_fields, before, after, before, after, factor)


def halo_pieces(x, axis, dim, width):
    size, length = (lax.axis_size(axis), x.shape[dim])
    up = [(i, (i + 1) % size) for i in range(size - 1)]
    down = [(j, i) for i, j in up]
    last = lax.slice_in_dim(x, length - width, length, axis=dim)
    leading = lax.slice_in_dim(x, 0, width, axis=dim)
    return lax.ppermute(last, axis, up), lax.ppermute(leading, axis, down)

def pick_matmul(values, pick):
    parts = []
    rest = values
    for _ in range(2):
        head = lax.reduce_precision(rest, exponent_bits=8, mantissa_bits=7)
        parts.append(head)
        rest = rest - head
    parts.append(rest)
    rows = values.shape[0]
    stacked = jnp.concatenate(parts, 0).astype(jnp.bfloat16)
    product = jnp.dot(stacked, pick, preferred_element_type=jnp.float32)
    return (product[:rows] + product[rows : 2 * rows]) + product[2 * rows :]


def local(
    spectrum, courant, group_ratio, ocean_currents, elevation, sea_mask, owner_tile, ocean_slot
):
    bin_count, row_count, columns = spectrum.shape
    cell_count = row_count * columns
    tile_count = lax.axis_size("tile")
    capacity = 2 * ((cell_count + tile_count - 1) // tile_count)
    ocean_cells = elevation.shape[0]
    first_bin = lax.axis_index("sect") * bin_count
    bin_ids = first_bin + jnp.arange(bin_count, dtype=jnp.int32)
    dir_ids = bin_ids // NFREQ
    freq_ids = bin_ids % NFREQ
    freq_pick = (freq_ids[:, None] == jnp.arange(NFREQ, dtype=jnp.int32)[None, :]).astype(
        jnp.float32
    )
    group_speed = jnp.sum(freq_pick * courant[None, :], 1)
    ratio_bin = jnp.sum(freq_pick * group_ratio[None, :], 1)
    angles = (dir_ids.astype(jnp.float32) + 0.5) * (2.0 * math.pi / NDIR)
    cos_dir = jnp.cos(angles)
    sin_dir = jnp.sin(angles)
    owners = owner_tile[:, 0]
    cell_ids = jnp.arange(owners.shape[0], dtype=jnp.int32)
    earlier = (cell_ids[None, :] < cell_ids[:, None]).astype(jnp.bfloat16)
    owner_pick = owners[:, None] == jnp.arange(tile_count, dtype=jnp.int32)[None, :]
    seen = jnp.dot(earlier, owner_pick.astype(jnp.bfloat16), preferred_element_type=jnp.float32)
    rank_in = jnp.sum(jnp.where(owner_pick, seen, 0.0), 1).astype(jnp.int32)
    position = owners * capacity + rank_in
    slot_ids = jnp.arange(tile_count * capacity, dtype=jnp.int32)
    requests = jnp.max(
        jnp.where(position[:, None] == slot_ids[None, :], ocean_slot[:, None], -1), 0
    )
    asked_slots = lax.all_to_all(
        requests.reshape(tile_count, capacity), "tile", split_axis=0, concat_axis=0, tiled=True
    )
    is_valid = asked_slots >= 0
    surface = jnp.concatenate([ocean_currents, elevation[None]], 0)
    ocean_ids = jnp.arange(ocean_cells, dtype=jnp.int32)
    slot_pick = (ocean_ids[:, None] == asked_slots.reshape(-1)[None, :]).astype(jnp.bfloat16)
    answer = pick_matmul(surface, slot_pick).reshape(3, tile_count, capacity)
    returned = lax.all_to_all(answer, "tile", split_axis=1, concat_axis=1, tiled=True)
    cell_pick = (slot_ids[:, None] == position[None, :]).astype(jnp.bfloat16)
    at_cells = pick_matmul(returned.reshape(3, tile_count * capacity), cell_pick)
    sea_float = sea_mask.astype(jnp.float32)
    flow_fields = jnp.concatenate([at_cells[:2].reshape(2, row_count, columns), sea_float[None]], 0)
    before, after = halo_pieces(jnp.concatenate([spectrum, flow_fields], 0), "tile", 1, STEPS)
    speeds = jnp.stack([group_speed * cos_dir, group_speed * sin_dir], 0)
    weights = jnp.stack(
        [
            ratio_bin * (1.0 + cos_dir * cos_dir) - 0.5,
            ratio_bin * cos_dir * sin_dir,
            ratio_bin * (1.0 + sin_dir * sin_dir) - 0.5,
        ],
        0,
    ) * (4.0 / (NDIR * NFREQ))
    factor = ((1.0 + at_cells[2]) * sea_float.reshape(-1)).reshape(row_count, columns)
    sect_count = lax.axis_size("sect")
    energy, partial_copies = propagate(
        speeds, weights, spectrum, flow_fields, before, after, factor, sect_count
    )
    every_part = lax.all_to_all(partial_copies, "sect", 0, 0, tiled=True)
    partial_value = every_part[0]
    for part in range(1, sect_count):
        partial_value = partial_value + every_part[part]
    partial_value = partial_value.reshape(3, cell_count)
    packed = pick_matmul(partial_value, cell_pick.T)
    arrived = lax.all_to_all(
        packed.reshape(3, tile_count, capacity), "tile", split_axis=1, concat_axis=1, tiled=True
    )
    summed = pick_matmul(
        jnp.concatenate([arrived.reshape(3, -1), jnp.ones_like(arrived.reshape(3, -1)[:1])], 0),
        slot_pick.T,
    )
    return (energy, summed[:3] / jnp.maximum(summed[3], 1.0)[None])


def solution(mesh):
    in_specs = (
        P("sect", "tile", None),
        P(),
        P(),
        P(None, "tile"),
        P("tile"),
        P("tile", None),
        P("tile", None),
        P("tile"),
    )
    out_specs = (P("sect", "tile", None), P(None, "tile"))
    return jax.shard_map(local, mesh=mesh, in_specs=in_specs, out_specs=out_specs, check_vma=False)
```
